256 devices in a mesh: row: 8 (over y, core), col: 8 (over z), layer: 4 (over x).
Axes of the slice: x: 4, y: 4, z: 8, core: 2. Of those that a mesh axis runs over, the one named last changes fastest.
Arguments:
- density: bfloat16 [8192, 8192], P(('col', 'layer'), 'row'), as said below
- pattern: int32 [64, 64], replicated, may hold values from 0 to 1, as said below
Outputs:
- purified: bfloat16 [8192, 8192], P(('col', 'layer'), 'row')
The draws below stay inside these ranges and needn't reach their ends.
Inputs may be any that keep to these rules, and one draw needn't show every extreme that they name: pattern is symmetric and every diagonal tile is occupied; in every tile row, each aligned group of 4 consecutive column tiles holds at most 2 occupied tiles, and the group that holds the diagonal tile holds exactly that many. density is symmetric and zero outside the occupied tiles of pattern.
All inputs are finite; a program needn't handle non-finite values.
Results may differ from the reference program's by a relative error of at most 0.008.
Values may be sent and summed in bfloat16 or wider, within the bound.
No kernel may reach another device: no remote copies, remote signals or barrier semaphores. Data moves between devices by JAX's collectives and lax.ppermute only.
A program may use at most 64 MiB of HBM per device.

```python
import jax
import jax.numpy as jnp

TILE = 128
GROUP = 4
N = 8192


def tile_pattern(key):
    blocks = N // TILE
    group_size = GROUP
    most_live = group_size // 2
    group_count = blocks // group_size
    subkeys = jax.random.split(jax.random.fold_in(key, 11), group_count * group_count)
    orders = jax.vmap(lambda single: jax.random.permutation(single, group_size))(subkeys)
    orders = orders.reshape(group_count, group_count, group_size).astype(jnp.int32)
    offsets = jax.random.randint(jax.random.fold_in(key, 12), (group_count, group_count), 0, group_size)
    amounts = jax.random.randint(jax.random.fold_in(key, 13), (group_count, group_count), 0, most_live + 1)
    groups = jnp.arange(group_count, dtype=jnp.int32)
    inside = jnp.arange(group_size, dtype=jnp.int32)
    moved = (inside[None, None, None, :] - orders[:, :, :, None] - offsets[:, :, None, None]) % group_size
    above_part = moved < amounts[:, :, None, None]
    below_part = jnp.transpose(above_part, (1, 0, 3, 2))
    distance = (inside[None, :] - inside[:, None]) % group_size
    within = (distance == 0) | (distance == group_size // 2) | (jnp.minimum(distance, group_size - distance) < group_size // 4)
    upper_side = groups[:, None] < groups[None, :]
    lower_side = groups[:, None] > groups[None, :]
    joined = jnp.where(upper_side[:, :, None, None], above_part, jnp.where(lower_side[:, :, None, None], below_part, within[None, None, :, :]))
    return jnp.transpose(joined, (0, 2, 1, 3)).reshape(blocks, blocks).astype(jnp.int32)


def draw_pattern(key, part):
    return tile_pattern(key)


def draw_density(key, part):
    occupied = jnp.repeat(jnp.repeat(tile_pattern(key), TILE, axis=0), TILE, axis=1) > 0
    random_part = jax.random.normal(jax.random.fold_in(key, 22), (N, N), jnp.float32)
    diagonal = jax.random.uniform(jax.random.fold_in(key, 33), (N,), jnp.float32, 0.2, 0.8)
    coupling = (random_part + random_part.T) * 0.5 ** 0.5 * (1.0 / N) ** 0.5
    matrix = jnp.where(occupied, coupling, 0.0) + jnp.diag(diagonal)
    return matrix.astype(jnp.bfloat16)


def setup_inputs(seed: int = 0) -> dict:
    splits = jax.random.split(jax.random.key(seed), 3)
    density = draw_density(jax.random.fold_in(splits[2], 71), 0)
    pattern = draw_pattern(jax.random.fold_in(splits[2], 71), 0)
    return {"density": density, "pattern": pattern}


def reference(density, pattern):
    occupied = jnp.repeat(jnp.repeat(pattern, TILE, axis=0), TILE, axis=1) > 0
    square = jnp.where(occupied, jnp.dot(density, density, preferred_element_type=jnp.float32), jnp.float32(0.0)).astype(jnp.bfloat16)
    cubic = jnp.where(occupied, jnp.dot(square, density, preferred_element_type=jnp.float32), jnp.float32(0.0))
    purified = 3.0 * square.astype(jnp.float32) - 2.0 * cubic
    return purified.astype(jnp.bfloat16)
```

```python
import functools

import jax
import jax.numpy as jnp
from jax import lax
from jax.experimental import pallas as pl
from jax.experimental.pallas import tpu as pltpu
from jax.sharding import PartitionSpec as P

TILE = 128
GROUP = 4
KEEP = 2
K_STEP_TILES = 16


def slot_of_tile(occ):
    count = occ.astype(jnp.int32)
    before = jnp.cumsum(count, axis=-1) - count
    return jnp.where(occ, before, KEEP).astype(jnp.int32)


def tile_of_slot(occ):
    slot = slot_of_tile(occ)
    tiles = jnp.arange(GROUP, dtype=jnp.int32)
    picks = [jnp.min(jnp.where(slot == s, tiles, GROUP), axis=-1) for s in range(KEEP)]
    return jnp.stack(picks, axis=-1).astype(jnp.int32)


def compress_kernel(src_ref, x_ref, o_ref):
    row_tiles = x_ref.shape[0] // TILE
    groups = x_ref.shape[1] // (GROUP * TILE)
    zero = jnp.zeros((TILE, TILE), x_ref.dtype)
    for i in range(row_tiles):
        rows = slice(i * TILE, (i + 1) * TILE)
        for g in range(groups):
            for s in range(KEEP):
                src = src_ref[(i * groups + g) * KEEP + s]
                cur = zero
                for t in range(GROUP):
                    col = (g * GROUP + t) * TILE
                    cur = jnp.where(src == t, x_ref[rows, col:col + TILE], cur)
                out = (g * KEEP + s) * TILE
                o_ref[rows, out:out + TILE] = cur


def compress(x, occ):
    rows, cols = x.shape
    src = tile_of_slot(occ).reshape(-1)
    return pl.pallas_call(
        compress_kernel,
        out_shape=jax.ShapeDtypeStruct((rows, cols * KEEP // GROUP), x.dtype),
        grid_spec=pltpu.PrefetchScalarGridSpec(
            num_scalar_prefetch=1,
            grid=(1,),
            in_specs=[pl.BlockSpec((rows, cols), lambda i, s: (0, 0))],
            out_specs=pl.BlockSpec((rows, cols * KEEP // GROUP), lambda i, s: (0, 0)),
        ),
    )(src, x)


def expand_into(dst, src_ref, sel_ref, sel_base, rows, groups):
    zero = jnp.zeros((TILE, TILE), src_ref.dtype)
    for g in range(groups):
        s0 = src_ref[rows, (g * KEEP) * TILE:(g * KEEP + 1) * TILE]
        s1 = src_ref[rows, (g * KEEP + 1) * TILE:(g * KEEP + 2) * TILE]
        for t in range(GROUP):
            sel = sel_ref[sel_base + g * GROUP + t]
            col = (g * GROUP + t) * TILE
            dst[rows, col:col + TILE] = jnp.where(sel == 0, s0, jnp.where(sel == 1, s1, zero))


def product_kernel(k_tiles, rsel_ref, csel_ref, rp_ref, cp_ref, o_ref, rpx, cpx, acc):
    step = pl.program_id(0)
    step_tiles = cp_ref.shape[0] // TILE
    col_groups = cp_ref.shape[1] // (KEEP * TILE)
    row_tiles = rp_ref.shape[0] // TILE
    for kt in range(step_tiles):
        expand_into(cpx, cp_ref, csel_ref, (step * step_tiles + kt) * col_groups * GROUP,
                    slice(kt * TILE, (kt + 1) * TILE), col_groups)
    for i in range(row_tiles):
        expand_into(rpx, rp_ref, rsel_ref, i * k_tiles + step * step_tiles,
                    slice(i * TILE, (i + 1) * TILE), step_tiles // GROUP)

    @pl.when(step == 0)
    def _():
        acc[...] = jnp.zeros_like(acc)

    acc[...] += jnp.dot(rpx[...], cpx[...], preferred_element_type=jnp.float32)

    @pl.when(step == pl.num_programs(0) - 1)
    def _():
        o_ref[...] = acc[...]


def product(packed_rows, packed_panel, rsel, csel):
    rows = packed_rows.shape[0]
    k = packed_panel.shape[0]
    cols = packed_panel.shape[1] * GROUP // KEEP
    k_tiles = k // TILE
    step_k = K_STEP_TILES * TILE
    return pl.pallas_call(
        functools.partial(product_kernel, k_tiles),
        out_shape=jax.ShapeDtypeStruct((rows, cols), jnp.float32),
        grid_spec=pltpu.PrefetchScalarGridSpec(
            num_scalar_prefetch=2,
            grid=(k // step_k,),
            in_specs=[
                pl.BlockSpec((rows, step_k * KEEP // GROUP), lambda s, r, c: (0, s)),
                pl.BlockSpec((step_k, packed_panel.shape[1]), lambda s, r, c: (s, 0)),
            ],
            out_specs=pl.BlockSpec((rows, cols), lambda s, r, c: (0, 0)),
            scratch_shapes=[
                pltpu.VMEM((rows, step_k), packed_rows.dtype),
                pltpu.VMEM((step_k, cols), packed_panel.dtype),
                pltpu.VMEM((rows, cols), jnp.float32),
            ],
        ),
        compiler_params=pltpu.CompilerParams(dimension_semantics=("arbitrary",)),
        cost_estimate=pl.CostEstimate(
            flops=2 * rows * k * cols,
            transcendentals=0,
            bytes_accessed=2 * (packed_rows.size + packed_panel.size) + 4 * rows * cols,
        ),
    )(rsel, csel, packed_rows, packed_panel)


def shards(density, pattern):
    row_count, col_width = density.shape
    layers = lax.axis_size("layer")
    row_tile0 = (lax.axis_index("col") * layers + lax.axis_index("layer")) * (row_count // TILE)
    col_tile0 = lax.axis_index("row") * (col_width // TILE)
    live = pattern > 0
    own_rows = lax.dynamic_slice_in_dim(live, row_tile0, row_count // TILE, axis=0)
    own_cols = lax.dynamic_slice_in_dim(live, col_tile0, col_width // TILE, axis=1)
    own = lax.dynamic_slice_in_dim(own_rows, col_tile0, col_width // TILE, axis=1)
    occupied = jnp.repeat(jnp.repeat(own, TILE, axis=0), TILE, axis=1)

    groups = lambda m: m.reshape(m.shape[0], m.shape[1] // GROUP, GROUP)
    own_occ = groups(own)
    rsel = slot_of_tile(groups(own_rows)).reshape(-1)
    csel = slot_of_tile(groups(own_cols)).reshape(-1)

    packed_panel = lax.all_gather(compress(density, own_occ), ("col", "layer"), axis=0, tiled=True)

    def masked_product(operand):
        packed_rows = lax.all_gather(compress(operand, own_occ), "row", axis=1, tiled=True)
        return jnp.where(occupied, product(packed_rows, packed_panel, rsel, csel), jnp.float32(0.0))

    square = masked_product(density).astype(jnp.bfloat16)
    cubic = masked_product(square)
    purified = 3.0 * square.astype(jnp.float32) - 2.0 * cubic
    return purified.astype(jnp.bfloat16)


def solution(mesh):
    return jax.shard_map(
        shards,
        mesh=mesh,
        in_specs=(P(("col", "layer"), "row"), P()),
        out_specs=P(("col", "layer"), "row"),
        check_vma=False,
    )
```

```python
import functools

import jax
import jax.numpy as jnp
from jax import lax
from jax.experimental import pallas as pl
from jax.experimental.pallas import tpu as pltpu
from jax.sharding import PartitionSpec as P

TILE = 128
GROUP = 4
KEEP = 2


def slot_of_tile(occ):
    count = occ.astype(jnp.int32)
    before = jnp.cumsum(count, axis=-1) - count
    return jnp.where(occ, before, KEEP).astype(jnp.int32)


def tile_of_slot(occ):
    slot = slot_of_tile(occ)
    tiles = jnp.arange(GROUP, dtype=jnp.int32)
    picks = [jnp.min(jnp.where(slot == s, tiles, GROUP), axis=-1) for s in range(KEEP)]
    return jnp.stack(picks, axis=-1).astype(jnp.int32)


def compress_kernel(src_ref, x_ref, o_ref):
    row_tiles = x_ref.shape[0] // TILE
    groups = x_ref.shape[1] // (GROUP * TILE)
    zero = jnp.zeros((TILE, TILE), x_ref.dtype)
    for i in range(row_tiles):
        rows = slice(i * TILE, (i + 1) * TILE)
        for g in range(groups):
            for s in range(KEEP):
                src = src_ref[(i * groups + g) * KEEP + s]
                cur = zero
                for t in range(GROUP):
                    col = (g * GROUP + t) * TILE
                    cur = jnp.where(src == t, x_ref[rows, col:col + TILE], cur)
                out = (g * KEEP + s) * TILE
                o_ref[rows, out:out + TILE] = cur


def compress(x, occ):
    rows, cols = x.shape
    src = tile_of_slot(occ).reshape(-1)
    return pl.pallas_call(
        compress_kernel,
        out_shape=jax.ShapeDtypeStruct((rows, cols * KEEP // GROUP), x.dtype),
        grid_spec=pltpu.PrefetchScalarGridSpec(
            num_scalar_prefetch=1,
            grid=(1,),
            in_specs=[pl.BlockSpec((rows, cols), lambda i, s: (0, 0))],
            out_specs=pl.BlockSpec((rows, cols * KEEP // GROUP), lambda i, s: (0, 0)),
        ),
    )(src, x)


def product_kernel(k_tiles, gblk_ref, rpos_ref, rsel_ref, csel_ref, rp_ref, cpa_ref, cpb_ref,
                   o_ref, rpx, cpx, acc):
    step = pl.program_id(0)
    step_tiles = cpa_ref.shape[0] // TILE
    row_tiles = rp_ref.shape[0] // TILE
    block = gblk_ref[step]
    for kt in range(step_tiles):
        rows = slice(kt * TILE, (kt + 1) * TILE)
        for g, cp_ref in enumerate((cpa_ref, cpb_ref)):
            expand_group(cpx, cp_ref, csel_ref, ((block * step_tiles + kt) * 2 + g) * GROUP, rows, 0, g)
    for i in range(row_tiles):
        rows = slice(i * TILE, (i + 1) * TILE)
        for q in range(step_tiles // GROUP):
            expand_group(rpx, rp_ref, rsel_ref, i * k_tiles + block * step_tiles + q * GROUP, rows, q, q)

    @pl.when(step == 0)
    def _():
        acc[...] = jnp.zeros_like(acc)

    acc[...] += jnp.dot(rpx[...], cpx[...], preferred_element_type=jnp.float32)

    @pl.when(step == pl.num_programs(0) - 1)
    def _():
        o_ref[...] = acc[...]


def expand_group(dst, src_ref, sel_ref, sel_base, rows, src_group, dst_group):
    zero = jnp.zeros((TILE, TILE), src_ref.dtype)
    base = src_group * KEEP * TILE
    s0 = src_ref[rows, base:base + TILE]
    s1 = src_ref[rows, base + TILE:base + 2 * TILE]
    for t in range(GROUP):
        sel = sel_ref[sel_base + t]
        col = (dst_group * GROUP + t) * TILE
        dst[rows, col:col + TILE] = jnp.where(sel == 0, s0, jnp.where(sel == 1, s1, zero))


def product(packed_rows, panel_a, panel_b, gblk, rpos, rsel, csel):
    blocks, rows, _ = packed_rows.shape
    step_k = panel_a.shape[1]
    cols = 2 * GROUP * TILE
    k_tiles = blocks * step_k // TILE
    return pl.pallas_call(
        functools.partial(product_kernel, k_tiles),
        out_shape=jax.ShapeDtypeStruct((rows, cols), jnp.float32),
        grid_spec=pltpu.PrefetchScalarGridSpec(
            num_scalar_prefetch=4,
            grid=(blocks,),
            in_specs=[
                pl.BlockSpec((None, rows, packed_rows.shape[2]), lambda s, g, p, r, c: (p[g[s]], 0, 0)),
                pl.BlockSpec((None, step_k, panel_a.shape[2]), lambda s, g, p, r, c: (s, 0, 0)),
                pl.BlockSpec((None, step_k, panel_b.shape[2]), lambda s, g, p, r, c: (s, 0, 0)),
            ],
            out_specs=pl.BlockSpec((rows, cols), lambda s, g, p, r, c: (0, 0)),
            scratch_shapes=[
                pltpu.VMEM((rows, step_k), packed_rows.dtype),
                pltpu.VMEM((step_k, cols), panel_a.dtype),
                pltpu.VMEM((rows, cols), jnp.float32),
            ],
        ),
        compiler_params=pltpu.CompilerParams(dimension_semantics=("arbitrary",)),
        cost_estimate=pl.CostEstimate(
            flops=2 * rows * blocks * step_k * cols,
            transcendentals=0,
            bytes_accessed=2 * (packed_rows.size + panel_a.size + panel_b.size) + 4 * rows * cols,
        ),
    )(gblk, rpos, rsel, csel, packed_rows, panel_a, panel_b)


def ring_gather(x, axis, stride=1):
    size = lax.axis_size(axis)
    n = size // stride
    fwd_perm = [(i, (i + stride) % size) for i in range(size)]
    bwd_perm = [(i, (i - stride) % size) for i in range(size)]
    blocks = [None] * n
    blocks[0] = x
    f, b = x, x
    half = n // 2
    for k in range(1, half):
        f = lax.ppermute(f, axis, fwd_perm)
        b = lax.ppermute(b, axis, bwd_perm)
        blocks[n - k] = f
        blocks[k] = b
    cut = x.shape[0] // 2
    top = lax.ppermute(f[:cut], axis, fwd_perm)
    bottom = lax.ppermute(b[cut:], axis, bwd_perm)
    blocks[half] = jnp.concatenate([top, bottom], axis=0)
    return blocks


def shards(density, pattern):
    row_count, col_width = density.shape
    layers = lax.axis_size("layer")
    cols_n = lax.axis_size("col")
    rows_n = lax.axis_size("row")
    c = lax.axis_index("col")
    l = lax.axis_index("layer")
    r = lax.axis_index("row")
    row_tile0 = (c * layers + l) * (row_count // TILE)
    col_tile0 = r * (col_width // TILE)
    live = pattern > 0
    own_rows = lax.dynamic_slice_in_dim(live, row_tile0, row_count // TILE, axis=0)
    own_cols = lax.dynamic_slice_in_dim(live, col_tile0, col_width // TILE, axis=1)
    own = lax.dynamic_slice_in_dim(own_rows, col_tile0, col_width // TILE, axis=1)
    occupied = jnp.repeat(jnp.repeat(own, TILE, axis=0), TILE, axis=1)

    groups = lambda m: m.reshape(m.shape[0], m.shape[1] // GROUP, GROUP)
    own_occ = groups(own)
    rsel = slot_of_tile(groups(own_rows)).reshape(-1)
    csel = slot_of_tile(groups(own_cols)).reshape(-1)

    packed = compress(density, own_occ)
    width = packed.shape[1] // 2
    part_a, part_b = packed[:, :width], packed[:, width:]
    along_col = jnp.stack(ring_gather(part_a, "col"))
    by_layer = jnp.roll(jnp.stack(ring_gather(along_col, "layer")), l, axis=0)
    panel_a = by_layer.transpose(1, 0, 2, 3).reshape(cols_n, layers * row_count, width)
    by_layer_b = jnp.roll(jnp.stack(ring_gather(part_b, "layer")), l, axis=0)
    piece_b = by_layer_b.reshape(layers * row_count, width)
    panel_b = jnp.stack(ring_gather(piece_b, "col"))

    steps = jnp.arange(cols_n, dtype=jnp.int32)
    gblk = (c + steps) % cols_n

    partner = [(i, i ^ 1) for i in range(rows_n)]
    half_n = rows_n // 2
    held = jnp.concatenate([(r + 2 * steps[:half_n]) % rows_n, ((r ^ 1) + 2 * steps[:half_n]) % rows_n])
    rpos = jnp.sum(jnp.where(held[None, :] == steps[:, None], steps[None, :], 0), axis=1).astype(jnp.int32)

    def masked_product(operand):
        mine = jnp.stack(ring_gather(compress(operand, own_occ), "row", stride=2))
        theirs = lax.ppermute(mine, "row", partner)
        packed_rows = jnp.concatenate([mine, theirs], axis=0)
        out = product(packed_rows, panel_a, panel_b, gblk, rpos, rsel, csel)
        return jnp.where(occupied, out, jnp.float32(0.0))

    square = masked_product(density).astype(jnp.bfloat16)
    cubic = masked_product(square)
    purified = 3.0 * square.astype(jnp.float32) - 2.0 * cubic
    return purified.astype(jnp.bfloat16)


def solution(mesh):
    return jax.shard_map(
        shards,
        mesh=mesh,
        in_specs=(P(("col", "layer"), "row"), P()),
        out_specs=P(("col", "layer"), "row"),
        check_vma=False,
    )
```

```python
import functools

import jax
import jax.numpy as jnp
from jax import lax
from jax.experimental import pallas as pl
from jax.experimental.pallas import tpu as pltpu
from jax.sharding import PartitionSpec as P

TILE = 128
GROUP = 4
KEEP = 2


def slot_of_tile(occ):
    count = occ.astype(jnp.int32)
    before = jnp.cumsum(count, axis=-1) - count
    return jnp.where(occ, before, KEEP).astype(jnp.int32)


def tile_of_slot(occ):
    slot = slot_of_tile(occ)
    tiles = jnp.arange(GROUP, dtype=jnp.int32)
    picks = [jnp.min(jnp.where(slot == s, tiles, GROUP), axis=-1) for s in range(KEEP)]
    return jnp.stack(picks, axis=-1).astype(jnp.int32)


def compress_kernel(src_ref, x_ref, o_ref):
    row_tiles = x_ref.shape[0] // TILE
    groups = x_ref.shape[1] // (GROUP * TILE)
    zero = jnp.zeros((TILE, TILE), x_ref.dtype)
    for i in range(row_tiles):
        rows = slice(i * TILE, (i + 1) * TILE)
        for g in range(groups):
            for s in range(KEEP):
                src = src_ref[(i * groups + g) * KEEP + s]
                cur = zero
                for t in range(GROUP):
                    col = (g * GROUP + t) * TILE
                    cur = jnp.where(src == t, x_ref[rows, col:col + TILE], cur)
                out = (g * KEEP + s) * TILE
                o_ref[rows, out:out + TILE] = cur


def compress(x, occ):
    rows, cols = x.shape
    src = tile_of_slot(occ).reshape(-1)
    return pl.pallas_call(
        compress_kernel,
        out_shape=jax.ShapeDtypeStruct((rows, cols * KEEP // GROUP), x.dtype),
        grid_spec=pltpu.PrefetchScalarGridSpec(
            num_scalar_prefetch=1,
            grid=(1,),
            in_specs=[pl.BlockSpec((rows, cols), lambda i, s: (0, 0))],
            out_specs=pl.BlockSpec((rows, cols * KEEP // GROUP), lambda i, s: (0, 0)),
        ),
    )(src, x)


def product_kernel(k_tiles, gblk_ref, rpos_ref, rsel_ref, csel_ref, rp_ref, cpa_ref, cpb_ref,
                   o_ref, rpx, cpx, acc):
    step = pl.program_id(0)
    step_tiles = cpa_ref.shape[0] // TILE
    row_tiles = rp_ref.shape[0] // TILE
    block = gblk_ref[step]
    def expand_panel_tile(kt, carry):
        rows = pl.ds(pl.multiple_of(kt * TILE, TILE), TILE)
        for g, cp_ref in enumerate((cpa_ref, cpb_ref)):
            expand_group(cpx, cp_ref, csel_ref, ((block * step_tiles + kt) * 2 + g) * GROUP, rows, 0, g)
        return carry

    lax.fori_loop(0, step_tiles, expand_panel_tile, 0)
    for i in range(row_tiles):
        rows = slice(i * TILE, (i + 1) * TILE)
        for q in range(step_tiles // GROUP):
            expand_group(rpx, rp_ref, rsel_ref, i * k_tiles + block * step_tiles + q * GROUP, rows, q, q)

    @pl.when(step == 0)
    def _():
        acc[...] = jnp.zeros_like(acc)

    acc[...] += jnp.dot(rpx[...], cpx[...], preferred_element_type=jnp.float32)

    @pl.when(step == pl.num_programs(0) - 1)
    def _():
        o_ref[...] = acc[...]


def expand_group(dst, src_ref, sel_ref, sel_base, rows, src_group, dst_group):
    zero = jnp.zeros((TILE, TILE), src_ref.dtype)
    base = src_group * KEEP * TILE
    s0 = src_ref[rows, base:base + TILE]
    s1 = src_ref[rows, base + TILE:base + 2 * TILE]
    for t in range(GROUP):
        sel = sel_ref[sel_base + t]
        col = (dst_group * GROUP + t) * TILE
        dst[rows, col:col + TILE] = jnp.where(sel == 0, s0, jnp.where(sel == 1, s1, zero))


def product(packed_rows, panel_a, panel_b, gblk, rpos, rsel, csel):
    blocks, rows, _ = packed_rows.shape
    step_k = panel_a.shape[1]
    cols = 2 * GROUP * TILE
    k_tiles = blocks * step_k // TILE
    return pl.pallas_call(
        functools.partial(product_kernel, k_tiles),
        out_shape=jax.ShapeDtypeStruct((rows, cols), jnp.float32),
        grid_spec=pltpu.PrefetchScalarGridSpec(
            num_scalar_prefetch=4,
            grid=(blocks,),
            in_specs=[
                pl.BlockSpec((None, rows, packed_rows.shape[2]), lambda s, g, p, r, c: (p[g[s]], 0, 0)),
                pl.BlockSpec((None, step_k, panel_a.shape[2]), lambda s, g, p, r, c: (s, 0, 0)),
                pl.BlockSpec((None, step_k, panel_b.shape[2]), lambda s, g, p, r, c: (s, 0, 0)),
            ],
            out_specs=pl.BlockSpec((rows, cols), lambda s, g, p, r, c: (0, 0)),
            scratch_shapes=[
                pltpu.VMEM((rows, step_k), packed_rows.dtype),
                pltpu.VMEM((step_k, cols), panel_a.dtype),
                pltpu.VMEM((rows, cols), jnp.float32),
            ],
        ),
        compiler_params=pltpu.CompilerParams(dimension_semantics=("arbitrary",)),
        cost_estimate=pl.CostEstimate(
            flops=2 * rows * blocks * step_k * cols,
            transcendentals=0,
            bytes_accessed=2 * (packed_rows.size + panel_a.size + panel_b.size) + 4 * rows * cols,
        ),
    )(gblk, rpos, rsel, csel, packed_rows, panel_a, panel_b)


def ring_gather(x, axis, stride=1):
    size = lax.axis_size(axis)
    n = size // stride
    fwd_perm = [(i, (i + stride) % size) for i in range(size)]
    bwd_perm = [(i, (i - stride) % size) for i in range(size)]
    blocks = [None] * n
    blocks[0] = x
    f, b = x, x
    half = n // 2
    for k in range(1, half):
        f = lax.ppermute(f, axis, fwd_perm)
        b = lax.ppermute(b, axis, bwd_perm)
        blocks[n - k] = f
        blocks[k] = b
    cut = x.shape[0] // 2
    top = lax.ppermute(f[:cut], axis, fwd_perm)
    bottom = lax.ppermute(b[cut:], axis, bwd_perm)
    blocks[half] = jnp.concatenate([top, bottom], axis=0)
    return blocks


def shards(density, pattern):
    row_count, col_width = density.shape
    layers = lax.axis_size("layer")
    cols_n = lax.axis_size("col")
    rows_n = lax.axis_size("row")
    c = lax.axis_index("col")
    l = lax.axis_index("layer")
    r = lax.axis_index("row")
    row_tile0 = (c * layers + l) * (row_count // TILE)
    col_tile0 = r * (col_width // TILE)
    live = pattern > 0
    own_rows = lax.dynamic_slice_in_dim(live, row_tile0, row_count // TILE, axis=0)
    own_cols = lax.dynamic_slice_in_dim(live, col_tile0, col_width // TILE, axis=1)
    own = lax.dynamic_slice_in_dim(own_rows, col_tile0, col_width // TILE, axis=1)
    occupied = jnp.repeat(jnp.repeat(own, TILE, axis=0), TILE, axis=1)

    groups = lambda m: m.reshape(m.shape[0], m.shape[1] // GROUP, GROUP)
    own_occ = groups(own)
    csel = slot_of_tile(groups(own_cols)).reshape(-1)

    packed = compress(density, own_occ)
    width = packed.shape[1] // 2
    part_a, part_b = packed[:, :width], packed[:, width:]
    along_col = jnp.stack(ring_gather(part_a, "col"))
    by_layer = jnp.roll(jnp.stack(ring_gather(along_col, "layer")), l, axis=0)
    panel_a = by_layer.transpose(1, 0, 2, 3).reshape(cols_n, layers * row_count, width)
    by_layer_b = jnp.roll(jnp.stack(ring_gather(part_b, "layer")), l, axis=0)
    piece_b = by_layer_b.reshape(layers * row_count, width)
    panel_b = jnp.stack(ring_gather(piece_b, "col"))

    steps = jnp.arange(cols_n, dtype=jnp.int32)
    gblk = (c + steps) % cols_n

    partner = [(i, i ^ 1) for i in range(rows_n)]
    half_n = rows_n // 2
    held = jnp.concatenate([(r + 2 * steps[:half_n]) % rows_n, ((r ^ 1) + 2 * steps[:half_n]) % rows_n])
    rpos = jnp.sum(jnp.where(held[None, :] == steps[:, None], steps[None, :], 0), axis=1).astype(jnp.int32)

    def gather_rows(packed):
        mine = jnp.stack(ring_gather(packed, "row", stride=2))
        theirs = lax.ppermute(mine, "row", partner)
        return jnp.concatenate([mine, theirs], axis=0)

    def masked_product(packed_rows, i):
        rsel = slot_of_tile(groups(own_rows[i:i + 1])).reshape(-1)
        out = product(packed_rows, panel_a, panel_b, gblk, rpos, rsel, csel)
        return jnp.where(occupied[i * TILE:(i + 1) * TILE], out, jnp.float32(0.0))

    density_rows = gather_rows(compress(density, own_occ))
    purified = []
    squares = []
    for i in range(row_count // TILE):
        square = masked_product(density_rows[:, i * TILE:(i + 1) * TILE], i).astype(jnp.bfloat16)
        squares.append((square, gather_rows(compress(square, own_occ[i:i + 1]))))
    for i, (square, square_rows) in enumerate(squares):
        cubic = masked_product(square_rows, i)
        purified.append((3.0 * square.astype(jnp.float32) - 2.0 * cubic).astype(jnp.bfloat16))
    return jnp.concatenate(purified, axis=0)


def solution(mesh):
    return jax.shard_map(
        shards,
        mesh=mesh,
        in_specs=(P(("col", "layer"), "row"), P()),
        out_specs=P(("col", "layer"), "row"),
        check_vma=False,
    )
```

```python
import functools

import jax
import jax.numpy as jnp
from jax import lax
from jax.experimental import pallas as pl
from jax.experimental.pallas import tpu as pltpu
from jax.sharding import PartitionSpec as P

TILE = 128
GROUP = 4
KEEP = 2


def slot_of_tile(occ):
    count = occ.astype(jnp.int32)
    before = jnp.cumsum(count, axis=-1) - count
    return jnp.where(occ, before, KEEP).astype(jnp.int32)


def tile_of_slot(occ):
    slot = slot_of_tile(occ)
    tiles = jnp.arange(GROUP, dtype=jnp.int32)
    picks = [jnp.min(jnp.where(slot == s, tiles, GROUP), axis=-1) for s in range(KEEP)]
    return jnp.stack(picks, axis=-1).astype(jnp.int32)


def compress_kernel(src_ref, x_ref, o_ref):
    row_tiles = x_ref.shape[0] // TILE
    groups = x_ref.shape[1] // (GROUP * TILE)
    zero = jnp.zeros((TILE, TILE), x_ref.dtype)
    for i in range(row_tiles):
        rows = slice(i * TILE, (i + 1) * TILE)
        for g in range(groups):
            for s in range(KEEP):
                src = src_ref[(i * groups + g) * KEEP + s]
                cur = zero
                for t in range(GROUP):
                    col = (g * GROUP + t) * TILE
                    cur = jnp.where(src == t, x_ref[rows, col:col + TILE], cur)
                out = (g * KEEP + s) * TILE
                o_ref[rows, out:out + TILE] = cur


def compress(x, occ):
    rows, cols = x.shape
    src = tile_of_slot(occ).reshape(-1)
    return pl.pallas_call(
        compress_kernel,
        out_shape=jax.ShapeDtypeStruct((rows, cols * KEEP // GROUP), x.dtype),
        grid_spec=pltpu.PrefetchScalarGridSpec(
            num_scalar_prefetch=1,
            grid=(1,),
            in_specs=[pl.BlockSpec((rows, cols), lambda i, s: (0, 0))],
            out_specs=pl.BlockSpec((rows, cols * KEEP // GROUP), lambda i, s: (0, 0)),
        ),
    )(src, x)


def product_kernel(k_tiles, finish_square, gblk_ref, rpos_ref, rsel_ref, csel_ref, own_ref, src_ref, rp_ref, cpa_ref,
                   cpb_ref, *rest):
    if finish_square:
        o_ref, packed_ref, rpx, cpx, acc = rest
    else:
        sq_ref, o_ref, rpx, cpx, acc = rest
    step = pl.program_id(0)
    step_tiles = cpa_ref.shape[0] // TILE
    row_tiles = rp_ref.shape[0] // TILE
    col_tiles = o_ref.shape[1] // TILE
    block = gblk_ref[step]

    def expand_panel_tile(kt, carry):
        rows = pl.ds(pl.multiple_of(kt * TILE, TILE), TILE)
        for g, cp_ref in enumerate((cpa_ref, cpb_ref)):
            expand_group(cpx, cp_ref, csel_ref, ((block * step_tiles + kt) * 2 + g) * GROUP, rows, 0, g)
        return carry

    lax.fori_loop(0, step_tiles, expand_panel_tile, 0)
    for i in range(row_tiles):
        rows = slice(i * TILE, (i + 1) * TILE)
        for q in range(step_tiles // GROUP):
            expand_group(rpx, rp_ref, rsel_ref, i * k_tiles + block * step_tiles + q * GROUP, rows, q, q)

    @pl.when(step == 0)
    def _():
        acc[...] = jnp.zeros_like(acc)

    acc[...] += jnp.dot(rpx[...], cpx[...], preferred_element_type=jnp.float32)

    @pl.when(step == pl.num_programs(0) - 1)
    def _():
        zero = jnp.zeros((TILE, TILE), jnp.float32)
        for i in range(row_tiles):
            rows = slice(i * TILE, (i + 1) * TILE)
            for j in range(col_tiles):
                cols = slice(j * TILE, (j + 1) * TILE)
                masked = jnp.where(own_ref[i * col_tiles + j] > 0, acc[rows, cols], zero)
                if finish_square:
                    o_ref[rows, cols] = masked.astype(o_ref.dtype)
                else:
                    purified = 3.0 * sq_ref[rows, cols].astype(jnp.float32) - 2.0 * masked
                    o_ref[rows, cols] = purified.astype(o_ref.dtype)
        if finish_square:
            groups = col_tiles // GROUP
            bzero = jnp.zeros((TILE, TILE), o_ref.dtype)
            for i in range(row_tiles):
                rows = slice(i * TILE, (i + 1) * TILE)
                for g in range(groups):
                    for s in range(KEEP):
                        src = src_ref[(i * groups + g) * KEEP + s]
                        cur = bzero
                        for t in range(GROUP):
                            col = (g * GROUP + t) * TILE
                            cur = jnp.where(src == t, o_ref[rows, col:col + TILE], cur)
                        out = (g * KEEP + s) * TILE
                        packed_ref[rows, out:out + TILE] = cur


def expand_group(dst, src_ref, sel_ref, sel_base, rows, src_group, dst_group):
    zero = jnp.zeros((TILE, TILE), src_ref.dtype)
    base = src_group * KEEP * TILE
    s0 = src_ref[rows, base:base + TILE]
    s1 = src_ref[rows, base + TILE:base + 2 * TILE]
    for t in range(GROUP):
        sel = sel_ref[sel_base + t]
        col = (dst_group * GROUP + t) * TILE
        dst[rows, col:col + TILE] = jnp.where(sel == 0, s0, jnp.where(sel == 1, s1, zero))


def product(packed_rows, panel_a, panel_b, gblk, rpos, rsel, csel, own, src, square=None):
    blocks, rows, _ = packed_rows.shape
    step_k = panel_a.shape[1]
    cols = 2 * GROUP * TILE
    k_tiles = blocks * step_k // TILE
    index = lambda s, g, p, r, c, o, q: (0, 0)
    in_specs = [
        pl.BlockSpec((None, rows, packed_rows.shape[2]), lambda s, g, p, r, c, o, q: (p[g[s]], 0, 0)),
        pl.BlockSpec((None, step_k, panel_a.shape[2]), lambda s, g, p, r, c, o, q: (s, 0, 0)),
        pl.BlockSpec((None, step_k, panel_b.shape[2]), lambda s, g, p, r, c, o, q: (s, 0, 0)),
    ]
    operands = [packed_rows, panel_a, panel_b]
    if square is None:
        out_shape = (jax.ShapeDtypeStruct((rows, cols), jnp.bfloat16),
                     jax.ShapeDtypeStruct((rows, cols * KEEP // GROUP), jnp.bfloat16))
        out_specs = (pl.BlockSpec((rows, cols), index), pl.BlockSpec((rows, cols * KEEP // GROUP), index))
    else:
        in_specs.append(pl.BlockSpec((rows, cols), index))
        operands.append(square)
        out_shape = jax.ShapeDtypeStruct((rows, cols), jnp.bfloat16)
        out_specs = pl.BlockSpec((rows, cols), index)
    return pl.pallas_call(
        functools.partial(product_kernel, k_tiles, square is None),
        out_shape=out_shape,
        grid_spec=pltpu.PrefetchScalarGridSpec(
            num_scalar_prefetch=6,
            grid=(blocks,),
            in_specs=in_specs,
            out_specs=out_specs,
            scratch_shapes=[
                pltpu.VMEM((rows, step_k), packed_rows.dtype),
                pltpu.VMEM((step_k, cols), panel_a.dtype),
                pltpu.VMEM((rows, cols), jnp.float32),
            ],
        ),
        compiler_params=pltpu.CompilerParams(dimension_semantics=("arbitrary",)),
        cost_estimate=pl.CostEstimate(
            flops=2 * rows * blocks * step_k * cols,
            transcendentals=0,
            bytes_accessed=2 * (packed_rows.size + panel_a.size + panel_b.size) + 4 * rows * cols,
        ),
    )(gblk, rpos, rsel, csel, own, src, *operands)


def ring_gather(x, axis, stride=1):
    size = lax.axis_size(axis)
    n = size // stride
    fwd_perm = [(i, (i + stride) % size) for i in range(size)]
    bwd_perm = [(i, (i - stride) % size) for i in range(size)]
    blocks = [None] * n
    blocks[0] = x
    f, b = x, x
    half = n // 2
    for k in range(1, half):
        f = lax.ppermute(f, axis, fwd_perm)
        b = lax.ppermute(b, axis, bwd_perm)
        blocks[n - k] = f
        blocks[k] = b
    cut = x.shape[0] // 2
    top = lax.ppermute(f[:cut], axis, fwd_perm)
    bottom = lax.ppermute(b[cut:], axis, bwd_perm)
    blocks[half] = jnp.concatenate([top, bottom], axis=0)
    return blocks


def shards(density, pattern):
    row_count, col_width = density.shape
    layers = lax.axis_size("layer")
    cols_n = lax.axis_size("col")
    rows_n = lax.axis_size("row")
    c = lax.axis_index("col")
    l = lax.axis_index("layer")
    r = lax.axis_index("row")
    row_tile0 = (c * layers + l) * (row_count // TILE)
    col_tile0 = r * (col_width // TILE)
    live = pattern > 0
    own_rows = lax.dynamic_slice_in_dim(live, row_tile0, row_count // TILE, axis=0)
    own_cols = lax.dynamic_slice_in_dim(live, col_tile0, col_width // TILE, axis=1)
    own = lax.dynamic_slice_in_dim(own_rows, col_tile0, col_width // TILE, axis=1)

    groups = lambda m: m.reshape(m.shape[0], m.shape[1] // GROUP, GROUP)
    own_occ = groups(own)
    rsel = slot_of_tile(groups(own_rows)).reshape(-1)
    csel = slot_of_tile(groups(own_cols)).reshape(-1)

    packed = compress(density, own_occ)
    width = packed.shape[1] // 2
    part_a, part_b = packed[:, :width], packed[:, width:]
    along_col = jnp.stack(ring_gather(part_a, "col"))
    by_layer = jnp.roll(jnp.stack(ring_gather(along_col, "layer")), l, axis=0)
    panel_a = by_layer.transpose(1, 0, 2, 3).reshape(cols_n, layers * row_count, width)
    by_layer_b = jnp.roll(jnp.stack(ring_gather(part_b, "layer")), l, axis=0)
    piece_b = by_layer_b.reshape(layers * row_count, width)
    panel_b = jnp.stack(ring_gather(piece_b, "col"))

    steps = jnp.arange(cols_n, dtype=jnp.int32)
    gblk = (c + steps) % cols_n

    partner = [(i, i ^ 1) for i in range(rows_n)]
    half_n = rows_n // 2
    held = jnp.concatenate([(r + 2 * steps[:half_n]) % rows_n, ((r ^ 1) + 2 * steps[:half_n]) % rows_n])
    rpos = jnp.sum(jnp.where(held[None, :] == steps[:, None], steps[None, :], 0), axis=1).astype(jnp.int32)

    own_flat = own.astype(jnp.int32).reshape(-1)
    own_src = tile_of_slot(own_occ).reshape(-1)

    def gather_rows(packed):
        mine = jnp.stack(ring_gather(packed, "row", stride=2))
        theirs = lax.ppermute(mine, "row", partner)
        return jnp.concatenate([mine, theirs], axis=0)

    tables = (gblk, rpos, rsel, csel, own_flat, own_src)
    square, packed_square = product(gather_rows(packed), panel_a, panel_b, *tables)
    return product(gather_rows(packed_square), panel_a, panel_b, *tables, square=square)


def solution(mesh):
    return jax.shard_map(
        shards,
        mesh=mesh,
        in_specs=(P(("col", "layer"), "row"), P()),
        out_specs=P(("col", "layer"), "row"),
        check_vma=False,
    )
```

```python
import functools

import jax
import jax.numpy as jnp
from jax import lax
from jax.experimental import pallas as pl
from jax.experimental.pallas import tpu as pltpu
from jax.sharding import PartitionSpec as P

TILE = 128
GROUP = 4
KEEP = 2


def slot_of_tile(occ):
    count = occ.astype(jnp.int32)
    before = jnp.cumsum(count, axis=-1) - count
    return jnp.where(occ, before, KEEP).astype(jnp.int32)


def tile_of_slot(occ):
    slot = slot_of_tile(occ)
    tiles = jnp.arange(GROUP, dtype=jnp.int32)
    picks = [jnp.min(jnp.where(slot == s, tiles, GROUP), axis=-1) for s in range(KEEP)]
    return jnp.stack(picks, axis=-1).astype(jnp.int32)


def compress_kernel(src_ref, x_ref, o_ref):
    row_tiles = x_ref.shape[0] // TILE
    groups = x_ref.shape[1] // (GROUP * TILE)
    zero = jnp.zeros((TILE, TILE), x_ref.dtype)
    for i in range(row_tiles):
        rows = slice(i * TILE, (i + 1) * TILE)
        for g in range(groups):
            for s in range(KEEP):
                src = src_ref[(i * groups + g) * KEEP + s]
                cur = zero
                for t in range(GROUP):
                    col = (g * GROUP + t) * TILE
                    cur = jnp.where(src == t, x_ref[rows, col:col + TILE], cur)
                out = (g * KEEP + s) * TILE
                o_ref[rows, out:out + TILE] = cur


def compress(x, occ):
    rows, cols = x.shape
    src = tile_of_slot(occ).reshape(-1)
    return pl.pallas_call(
        compress_kernel,
        out_shape=jax.ShapeDtypeStruct((rows, cols * KEEP // GROUP), x.dtype),
        grid_spec=pltpu.PrefetchScalarGridSpec(
            num_scalar_prefetch=1,
            grid=(1,),
            in_specs=[pl.BlockSpec((rows, cols), lambda i, s: (0, 0))],
            out_specs=pl.BlockSpec((rows, cols * KEEP // GROUP), lambda i, s: (0, 0)),
        ),
    )(src, x)


def product_kernel(k_tiles, finish_square, gblk_ref, rpos_ref, rsel_ref, csel_ref, own_ref, src_ref, rp_ref, cpa_ref,
                   cpb_ref, *rest):
    if finish_square:
        o_ref, packed_ref, rpx, cpx, acc = rest
    else:
        sq_ref, o_ref, rpx, cpx, acc = rest
    step = pl.program_id(0)
    step_tiles = cpa_ref.shape[0] // TILE
    row_tiles = rp_ref.shape[0] // TILE
    col_tiles = o_ref.shape[1] // TILE
    block = gblk_ref[step]

    def expand_panel_tile(kt, carry):
        rows = pl.ds(pl.multiple_of(kt * TILE, TILE), TILE)
        for g, cp_ref in enumerate((cpa_ref, cpb_ref)):
            expand_group(cpx, cp_ref, csel_ref, ((block * step_tiles + kt) * 2 + g) * GROUP, rows, 0, g)
        return carry

    lax.fori_loop(0, step_tiles, expand_panel_tile, 0)
    for i in range(row_tiles):
        rows = slice(i * TILE, (i + 1) * TILE)
        for q in range(step_tiles // GROUP):
            expand_group(rpx, rp_ref, rsel_ref, i * k_tiles + block * step_tiles + q * GROUP, rows, q, q)

    @pl.when(step == 0)
    def _():
        acc[...] = jnp.zeros_like(acc)

    acc[...] += jnp.dot(rpx[...], cpx[...], preferred_element_type=jnp.float32)

    @pl.when(step == pl.num_programs(0) - 1)
    def _():
        zero = jnp.zeros((TILE, TILE), jnp.float32)
        for i in range(row_tiles):
            rows = slice(i * TILE, (i + 1) * TILE)
            for j in range(col_tiles):
                cols = slice(j * TILE, (j + 1) * TILE)
                masked = jnp.where(own_ref[i * col_tiles + j] > 0, acc[rows, cols], zero)
                if finish_square:
                    o_ref[rows, cols] = masked.astype(o_ref.dtype)
                else:
                    purified = 3.0 * sq_ref[rows, cols].astype(jnp.float32) - 2.0 * masked
                    o_ref[rows, cols] = purified.astype(o_ref.dtype)
        if finish_square:
            groups = col_tiles // GROUP
            bzero = jnp.zeros((TILE, TILE), o_ref.dtype)
            for i in range(row_tiles):
                rows = slice(i * TILE, (i + 1) * TILE)
                for g in range(groups):
                    for s in range(KEEP):
                        src = src_ref[(i * groups + g) * KEEP + s]
                        cur = bzero
                        for t in range(GROUP):
                            col = (g * GROUP + t) * TILE
                            cur = jnp.where(src == t, o_ref[rows, col:col + TILE], cur)
                        out = (g * KEEP + s) * TILE
                        packed_ref[rows, out:out + TILE] = cur


def expand_group(dst, src_ref, sel_ref, sel_base, rows, src_group, dst_group):
    base = src_group * KEEP * TILE
    for t in range(GROUP):
        sel = sel_ref[sel_base + t]
        col = (dst_group * GROUP + t) * TILE
        for s in range(KEEP):
            @pl.when(sel == s)
            def _():
                dst[rows, col:col + TILE] = src_ref[rows, base + s * TILE:base + (s + 1) * TILE]

        @pl.when(sel == KEEP)
        def _():
            dst[rows, col:col + TILE] = jnp.zeros((TILE, TILE), dst.dtype)


def product(packed_rows, panel_a, panel_b, gblk, rpos, rsel, csel, own, src, square=None):
    blocks, rows, _ = packed_rows.shape
    step_k = panel_a.shape[1]
    cols = 2 * GROUP * TILE
    k_tiles = blocks * step_k // TILE
    index = lambda s, g, p, r, c, o, q: (0, 0)
    in_specs = [
        pl.BlockSpec((None, rows, packed_rows.shape[2]), lambda s, g, p, r, c, o, q: (p[g[s]], 0, 0)),
        pl.BlockSpec((None, step_k, panel_a.shape[2]), lambda s, g, p, r, c, o, q: (s, 0, 0)),
        pl.BlockSpec((None, step_k, panel_b.shape[2]), lambda s, g, p, r, c, o, q: (s, 0, 0)),
    ]
    operands = [packed_rows, panel_a, panel_b]
    if square is None:
        out_shape = (jax.ShapeDtypeStruct((rows, cols), jnp.bfloat16),
                     jax.ShapeDtypeStruct((rows, cols * KEEP // GROUP), jnp.bfloat16))
        out_specs = (pl.BlockSpec((rows, cols), index), pl.BlockSpec((rows, cols * KEEP // GROUP), index))
    else:
        in_specs.append(pl.BlockSpec((rows, cols), index))
        operands.append(square)
        out_shape = jax.ShapeDtypeStruct((rows, cols), jnp.bfloat16)
        out_specs = pl.BlockSpec((rows, cols), index)
    return pl.pallas_call(
        functools.partial(product_kernel, k_tiles, square is None),
        out_shape=out_shape,
        grid_spec=pltpu.PrefetchScalarGridSpec(
            num_scalar_prefetch=6,
            grid=(blocks,),
            in_specs=in_specs,
            out_specs=out_specs,
            scratch_shapes=[
                pltpu.VMEM((rows, step_k), packed_rows.dtype),
                pltpu.VMEM((step_k, cols), panel_a.dtype),
                pltpu.VMEM((rows, cols), jnp.float32),
            ],
        ),
        compiler_params=pltpu.CompilerParams(dimension_semantics=("arbitrary",)),
        cost_estimate=pl.CostEstimate(
            flops=2 * rows * blocks * step_k * cols,
            transcendentals=0,
            bytes_accessed=2 * (packed_rows.size + panel_a.size + panel_b.size) + 4 * rows * cols,
        ),
    )(gblk, rpos, rsel, csel, own, src, *operands)


def ring_gather(x, axis, stride=1):
    size = lax.axis_size(axis)
    n = size // stride
    fwd_perm = [(i, (i + stride) % size) for i in range(size)]
    bwd_perm = [(i, (i - stride) % size) for i in range(size)]
    blocks = [None] * n
    blocks[0] = x
    f, b = x, x
    half = n // 2
    for k in range(1, half):
        f = lax.ppermute(f, axis, fwd_perm)
        b = lax.ppermute(b, axis, bwd_perm)
        blocks[n - k] = f
        blocks[k] = b
    cut = x.shape[0] // 2
    top = lax.ppermute(f[:cut], axis, fwd_perm)
    bottom = lax.ppermute(b[cut:], axis, bwd_perm)
    blocks[half] = jnp.concatenate([top, bottom], axis=0)
    return blocks


def shards(density, pattern):
    row_count, col_width = density.shape
    layers = lax.axis_size("layer")
    cols_n = lax.axis_size("col")
    rows_n = lax.axis_size("row")
    c = lax.axis_index("col")
    l = lax.axis_index("layer")
    r = lax.axis_index("row")
    row_tile0 = (c * layers + l) * (row_count // TILE)
    col_tile0 = r * (col_width // TILE)
    live = pattern > 0
    own_rows = lax.dynamic_slice_in_dim(live, row_tile0, row_count // TILE, axis=0)
    own_cols = lax.dynamic_slice_in_dim(live, col_tile0, col_width // TILE, axis=1)
    own = lax.dynamic_slice_in_dim(own_rows, col_tile0, col_width // TILE, axis=1)

    groups = lambda m: m.reshape(m.shape[0], m.shape[1] // GROUP, GROUP)
    own_occ = groups(own)
    rsel = slot_of_tile(groups(own_rows)).reshape(-1)
    csel = slot_of_tile(groups(own_cols)).reshape(-1)

    packed = compress(density, own_occ)
    width = packed.shape[1] // 2
    part_a, part_b = packed[:, :width], packed[:, width:]
    along_col = jnp.stack(ring_gather(part_a, "col"))
    by_layer = jnp.roll(jnp.stack(ring_gather(along_col, "layer")), l, axis=0)
    panel_a = by_layer.transpose(1, 0, 2, 3).reshape(cols_n, layers * row_count, width)
    by_layer_b = jnp.roll(jnp.stack(ring_gather(part_b, "layer")), l, axis=0)
    piece_b = by_layer_b.reshape(layers * row_count, width)
    panel_b = jnp.stack(ring_gather(piece_b, "col"))

    steps = jnp.arange(cols_n, dtype=jnp.int32)
    gblk = (c + steps) % cols_n

    partner = [(i, i ^ 1) for i in range(rows_n)]
    half_n = rows_n // 2
    held = jnp.concatenate([(r + 2 * steps[:half_n]) % rows_n, ((r ^ 1) + 2 * steps[:half_n]) % rows_n])
    rpos = jnp.sum(jnp.where(held[None, :] == steps[:, None], steps[None, :], 0), axis=1).astype(jnp.int32)

    own_flat = own.astype(jnp.int32).reshape(-1)
    own_src = tile_of_slot(own_occ).reshape(-1)

    def gather_rows(packed):
        mine = jnp.stack(ring_gather(packed, "row", stride=2))
        theirs = lax.ppermute(mine, "row", partner)
        return jnp.concatenate([mine, theirs], axis=0)

    tables = (gblk, rpos, rsel, csel, own_flat, own_src)
    square, packed_square = product(gather_rows(packed), panel_a, panel_b, *tables)
    return product(gather_rows(packed_square), panel_a, panel_b, *tables, square=square)


def solution(mesh):
    return jax.shard_map(
        shards,
        mesh=mesh,
        in_specs=(P(("col", "layer"), "row"), P()),
        out_specs=P(("col", "layer"), "row"),
        check_vma=False,
    )
```

```python
import functools

import jax
import jax.numpy as jnp
from jax import lax
from jax.experimental import pallas as pl
from jax.experimental.pallas import tpu as pltpu
from jax.sharding import PartitionSpec as P

TILE = 128
GROUP = 4
KEEP = 2


def slot_of_tile(occ):
    count = occ.astype(jnp.int32)
    before = jnp.cumsum(count, axis=-1) - count
    return jnp.where(occ, before, KEEP).astype(jnp.int32)


def tile_of_slot(occ):
    slot = slot_of_tile(occ)
    tiles = jnp.arange(GROUP, dtype=jnp.int32)
    picks = [jnp.min(jnp.where(slot == s, tiles, GROUP), axis=-1) for s in range(KEEP)]
    return jnp.stack(picks, axis=-1).astype(jnp.int32)


def compress_kernel(src_ref, x_ref, o_ref):
    row_tiles = x_ref.shape[0] // TILE
    groups = x_ref.shape[1] // (GROUP * TILE)
    zero = jnp.zeros((TILE, TILE), x_ref.dtype)
    for i in range(row_tiles):
        rows = slice(i * TILE, (i + 1) * TILE)
        for g in range(groups):
            for s in range(KEEP):
                src = src_ref[(i * groups + g) * KEEP + s]
                cur = zero
                for t in range(GROUP):
                    col = (g * GROUP + t) * TILE
                    cur = jnp.where(src == t, x_ref[rows, col:col + TILE], cur)
                out = (g * KEEP + s) * TILE
                o_ref[rows, out:out + TILE] = cur


def compress(x, occ):
    rows, cols = x.shape
    src = tile_of_slot(occ).reshape(-1)
    return pl.pallas_call(
        compress_kernel,
        out_shape=jax.ShapeDtypeStruct((rows, cols * KEEP // GROUP), x.dtype),
        grid_spec=pltpu.PrefetchScalarGridSpec(
            num_scalar_prefetch=1,
            grid=(1,),
            in_specs=[pl.BlockSpec((rows, cols), lambda i, s: (0, 0))],
            out_specs=pl.BlockSpec((rows, cols * KEEP // GROUP), lambda i, s: (0, 0)),
        ),
    )(src, x)


def panel_kernel(gblk_ref, csel_ref, cpa_ref, cpb_ref, o_ref):
    step_tiles = cpa_ref.shape[0] // TILE
    block = gblk_ref[pl.program_id(0)]

    def expand_panel_tile(kt, carry):
        rows = pl.ds(pl.multiple_of(kt * TILE, TILE), TILE)
        for g, cp_ref in enumerate((cpa_ref, cpb_ref)):
            expand_group(o_ref, cp_ref, csel_ref, ((block * step_tiles + kt) * 2 + g) * GROUP, rows, 0, g)
        return carry

    lax.fori_loop(0, step_tiles, expand_panel_tile, 0)


def expand_panel(panel_a, panel_b, gblk, csel):
    blocks, step_k, width = panel_a.shape
    cols = 2 * GROUP * TILE
    return pl.pallas_call(
        panel_kernel,
        out_shape=jax.ShapeDtypeStruct((blocks, step_k, cols), panel_a.dtype),
        grid_spec=pltpu.PrefetchScalarGridSpec(
            num_scalar_prefetch=2,
            grid=(blocks,),
            in_specs=[pl.BlockSpec((None, step_k, width), lambda s, g, c: (s, 0, 0))] * 2,
            out_specs=pl.BlockSpec((None, step_k, cols), lambda s, g, c: (s, 0, 0)),
        ),
        compiler_params=pltpu.CompilerParams(dimension_semantics=("arbitrary",)),
        cost_estimate=pl.CostEstimate(
            flops=0, transcendentals=0, bytes_accessed=2 * (panel_a.size + panel_b.size + blocks * step_k * cols)),
    )(gblk, csel, panel_a, panel_b)


def product_kernel(k_tiles, finish_square, gblk_ref, rpos_ref, rsel_ref, own_ref, src_ref, rp_ref, cp_ref,
                   *rest):
    if finish_square:
        o_ref, packed_ref, rpx, acc = rest
    else:
        sq_ref, o_ref, rpx, acc = rest
    step = pl.program_id(0)
    step_tiles = cp_ref.shape[0] // TILE
    row_tiles = rp_ref.shape[0] // TILE
    col_tiles = o_ref.shape[1] // TILE
    block = gblk_ref[step]

    for i in range(row_tiles):
        rows = slice(i * TILE, (i + 1) * TILE)
        for q in range(step_tiles // GROUP):
            expand_group(rpx, rp_ref, rsel_ref, i * k_tiles + block * step_tiles + q * GROUP, rows, q, q)

    @pl.when(step == 0)
    def _():
        acc[...] = jnp.zeros_like(acc)

    acc[...] += jnp.dot(rpx[...], cp_ref[...], preferred_element_type=jnp.float32)

    @pl.when(step == pl.num_programs(0) - 1)
    def _():
        zero = jnp.zeros((TILE, TILE), jnp.float32)
        for i in range(row_tiles):
            rows = slice(i * TILE, (i + 1) * TILE)
            for j in range(col_tiles):
                cols = slice(j * TILE, (j + 1) * TILE)
                masked = jnp.where(own_ref[i * col_tiles + j] > 0, acc[rows, cols], zero)
                if finish_square:
                    o_ref[rows, cols] = masked.astype(o_ref.dtype)
                else:
                    purified = 3.0 * sq_ref[rows, cols].astype(jnp.float32) - 2.0 * masked
                    o_ref[rows, cols] = purified.astype(o_ref.dtype)
        if finish_square:
            groups = col_tiles // GROUP
            bzero = jnp.zeros((TILE, TILE), o_ref.dtype)
            for i in range(row_tiles):
                rows = slice(i * TILE, (i + 1) * TILE)
                for g in range(groups):
                    for s in range(KEEP):
                        src = src_ref[(i * groups + g) * KEEP + s]
                        cur = bzero
                        for t in range(GROUP):
                            col = (g * GROUP + t) * TILE
                            cur = jnp.where(src == t, o_ref[rows, col:col + TILE], cur)
                        out = (g * KEEP + s) * TILE
                        packed_ref[rows, out:out + TILE] = cur


def expand_group(dst, src_ref, sel_ref, sel_base, rows, src_group, dst_group):
    zero = jnp.zeros((TILE, TILE), src_ref.dtype)
    base = src_group * KEEP * TILE
    s0 = src_ref[rows, base:base + TILE]
    s1 = src_ref[rows, base + TILE:base + 2 * TILE]
    for t in range(GROUP):
        sel = sel_ref[sel_base + t]
        col = (dst_group * GROUP + t) * TILE
        dst[rows, col:col + TILE] = jnp.where(sel == 0, s0, jnp.where(sel == 1, s1, zero))


def product(packed_rows, panel, gblk, rpos, rsel, own, src, square=None):
    blocks, rows, _ = packed_rows.shape
    step_k, cols = panel.shape[1:]
    k_tiles = blocks * step_k // TILE
    index = lambda s, g, p, r, o, q: (0, 0)
    in_specs = [
        pl.BlockSpec((None, rows, packed_rows.shape[2]), lambda s, g, p, r, o, q: (p[g[s]], 0, 0)),
        pl.BlockSpec((None, step_k, cols), lambda s, g, p, r, o, q: (s, 0, 0)),
    ]
    operands = [packed_rows, panel]
    if square is None:
        out_shape = (jax.ShapeDtypeStruct((rows, cols), jnp.bfloat16),
                     jax.ShapeDtypeStruct((rows, cols * KEEP // GROUP), jnp.bfloat16))
        out_specs = (pl.BlockSpec((rows, cols), index), pl.BlockSpec((rows, cols * KEEP // GROUP), index))
    else:
        in_specs.append(pl.BlockSpec((rows, cols), index))
        operands.append(square)
        out_shape = jax.ShapeDtypeStruct((rows, cols), jnp.bfloat16)
        out_specs = pl.BlockSpec((rows, cols), index)
    return pl.pallas_call(
        functools.partial(product_kernel, k_tiles, square is None),
        out_shape=out_shape,
        grid_spec=pltpu.PrefetchScalarGridSpec(
            num_scalar_prefetch=5,
            grid=(blocks,),
            in_specs=in_specs,
            out_specs=out_specs,
            scratch_shapes=[
                pltpu.VMEM((rows, step_k), packed_rows.dtype),
                pltpu.VMEM((rows, cols), jnp.float32),
            ],
        ),
        compiler_params=pltpu.CompilerParams(dimension_semantics=("arbitrary",)),
        cost_estimate=pl.CostEstimate(
            flops=2 * rows * blocks * step_k * cols,
            transcendentals=0,
            bytes_accessed=2 * (packed_rows.size + panel.size) + 4 * rows * cols,
        ),
    )(gblk, rpos, rsel, own, src, *operands)


def ring_gather(x, axis, stride=1):
    size = lax.axis_size(axis)
    n = size // stride
    fwd_perm = [(i, (i + stride) % size) for i in range(size)]
    bwd_perm = [(i, (i - stride) % size) for i in range(size)]
    blocks = [None] * n
    blocks[0] = x
    f, b = x, x
    half = n // 2
    for k in range(1, half):
        f = lax.ppermute(f, axis, fwd_perm)
        b = lax.ppermute(b, axis, bwd_perm)
        blocks[n - k] = f
        blocks[k] = b
    cut = x.shape[0] // 2
    top = lax.ppermute(f[:cut], axis, fwd_perm)
    bottom = lax.ppermute(b[cut:], axis, bwd_perm)
    blocks[half] = jnp.concatenate([top, bottom], axis=0)
    return blocks


def shards(density, pattern):
    row_count, col_width = density.shape
    layers = lax.axis_size("layer")
    cols_n = lax.axis_size("col")
    rows_n = lax.axis_size("row")
    c = lax.axis_index("col")
    l = lax.axis_index("layer")
    r = lax.axis_index("row")
    row_tile0 = (c * layers + l) * (row_count // TILE)
    col_tile0 = r * (col_width // TILE)
    live = pattern > 0
    own_rows = lax.dynamic_slice_in_dim(live, row_tile0, row_count // TILE, axis=0)
    own_cols = lax.dynamic_slice_in_dim(live, col_tile0, col_width // TILE, axis=1)
    own = lax.dynamic_slice_in_dim(own_rows, col_tile0, col_width // TILE, axis=1)

    groups = lambda m: m.reshape(m.shape[0], m.shape[1] // GROUP, GROUP)
    own_occ = groups(own)
    rsel = slot_of_tile(groups(own_rows)).reshape(-1)
    csel = slot_of_tile(groups(own_cols)).reshape(-1)

    packed = compress(density, own_occ)
    width = packed.shape[1] // 2
    part_a, part_b = packed[:, :width], packed[:, width:]
    along_col = jnp.stack(ring_gather(part_a, "col"))
    by_layer = jnp.roll(jnp.stack(ring_gather(along_col, "layer")), l, axis=0)
    panel_a = by_layer.transpose(1, 0, 2, 3).reshape(cols_n, layers * row_count, width)
    by_layer_b = jnp.roll(jnp.stack(ring_gather(part_b, "layer")), l, axis=0)
    piece_b = by_layer_b.reshape(layers * row_count, width)
    panel_b = jnp.stack(ring_gather(piece_b, "col"))

    steps = jnp.arange(cols_n, dtype=jnp.int32)
    gblk = (c + steps) % cols_n

    partner = [(i, i ^ 1) for i in range(rows_n)]
    half_n = rows_n // 2
    held = jnp.concatenate([(r + 2 * steps[:half_n]) % rows_n, ((r ^ 1) + 2 * steps[:half_n]) % rows_n])
    rpos = jnp.sum(jnp.where(held[None, :] == steps[:, None], steps[None, :], 0), axis=1).astype(jnp.int32)

    own_flat = own.astype(jnp.int32).reshape(-1)
    own_src = tile_of_slot(own_occ).reshape(-1)

    def gather_rows(packed):
        mine = jnp.stack(ring_gather(packed, "row", stride=2))
        theirs = lax.ppermute(mine, "row", partner)
        return jnp.concatenate([mine, theirs], axis=0)

    panel = expand_panel(panel_a, panel_b, gblk, csel)
    tables = (gblk, rpos, rsel, own_flat, own_src)
    square, packed_square = product(gather_rows(packed), panel, *tables)
    return product(gather_rows(packed_square), panel, *tables, square=square)


def solution(mesh):
    return jax.shard_map(
        shards,
        mesh=mesh,
        in_specs=(P(("col", "layer"), "row"), P()),
        out_specs=P(("col", "layer"), "row"),
        check_vma=False,
    )
```

```python
import functools

import jax
import jax.numpy as jnp
from jax import lax
from jax.experimental import pallas as pl
from jax.experimental.pallas import tpu as pltpu
from jax.sharding import PartitionSpec as P

TILE = 128
GROUP = 4
KEEP = 2


def slot_of_tile(occ):
    count = occ.astype(jnp.int32)
    before = jnp.cumsum(count, axis=-1) - count
    return jnp.where(occ, before, KEEP).astype(jnp.int32)


def tile_of_slot(occ):
    slot = slot_of_tile(occ)
    tiles = jnp.arange(GROUP, dtype=jnp.int32)
    picks = [jnp.min(jnp.where(slot == s, tiles, GROUP), axis=-1) for s in range(KEEP)]
    return jnp.stack(picks, axis=-1).astype(jnp.int32)


def compress_kernel(src_ref, x_ref, o_ref):
    row_tiles = x_ref.shape[0] // TILE
    groups = x_ref.shape[1] // (GROUP * TILE)
    zero = jnp.zeros((TILE, TILE), x_ref.dtype)
    for i in range(row_tiles):
        rows = slice(i * TILE, (i + 1) * TILE)
        for g in range(groups):
            for s in range(KEEP):
                src = src_ref[(i * groups + g) * KEEP + s]
                cur = zero
                for t in range(GROUP):
                    col = (g * GROUP + t) * TILE
                    cur = jnp.where(src == t, x_ref[rows, col:col + TILE], cur)
                out = (g * KEEP + s) * TILE
                o_ref[rows, out:out + TILE] = cur


def compress(x, occ):
    rows, cols = x.shape
    src = tile_of_slot(occ).reshape(-1)
    return pl.pallas_call(
        compress_kernel,
        out_shape=jax.ShapeDtypeStruct((rows, cols * KEEP // GROUP), x.dtype),
        grid_spec=pltpu.PrefetchScalarGridSpec(
            num_scalar_prefetch=1,
            grid=(1,),
            in_specs=[pl.BlockSpec((rows, cols), lambda i, s: (0, 0))],
            out_specs=pl.BlockSpec((rows, cols * KEEP // GROUP), lambda i, s: (0, 0)),
        ),
    )(src, x)


def product_kernel(k_tiles, finish_square, gblk_ref, rpos_ref, rsel_ref, csel_ref, own_ref, src_ref, rp_ref, cpa_ref,
                   cpb_ref, *rest):
    if finish_square:
        o_ref, packed_ref, rpx, cpx, acc = rest
    else:
        sq_ref, o_ref, rpx, cpx, acc = rest
    step = pl.program_id(0)
    step_tiles = cpa_ref.shape[0] // TILE
    row_tiles = rp_ref.shape[0] // TILE
    col_tiles = o_ref.shape[1] // TILE
    block = gblk_ref[step]

    def expand_panel_tile(kt, carry):
        rows = pl.ds(pl.multiple_of(kt * TILE, TILE), TILE)
        for g, cp_ref in enumerate((cpa_ref, cpb_ref)):
            expand_group(cpx, cp_ref, csel_ref, ((block * step_tiles + kt) * 2 + g) * GROUP, rows, 0, g)
        return carry

    lax.fori_loop(0, step_tiles, expand_panel_tile, 0)
    for i in range(row_tiles):
        rows = slice(i * TILE, (i + 1) * TILE)
        for q in range(step_tiles // GROUP):
            expand_group(rpx, rp_ref, rsel_ref, i * k_tiles + block * step_tiles + q * GROUP, rows, q, q)

    @pl.when(step == 0)
    def _():
        acc[...] = jnp.zeros_like(acc)

    acc[...] += jnp.dot(rpx[...], cpx[...], preferred_element_type=jnp.float32)

    @pl.when(step == pl.num_programs(0) - 1)
    def _():
        zero = jnp.zeros((TILE, TILE), jnp.float32)
        for i in range(row_tiles):
            rows = slice(i * TILE, (i + 1) * TILE)
            for j in range(col_tiles):
                cols = slice(j * TILE, (j + 1) * TILE)
                masked = jnp.where(own_ref[i * col_tiles + j] > 0, acc[rows, cols], zero)
                if finish_square:
                    o_ref[rows, cols] = masked.astype(o_ref.dtype)
                else:
                    purified = 3.0 * sq_ref[rows, cols].astype(jnp.float32) - 2.0 * masked
                    o_ref[rows, cols] = purified.astype(o_ref.dtype)
        if finish_square:
            groups = col_tiles // GROUP
            bzero = jnp.zeros((TILE, TILE), o_ref.dtype)
            for i in range(row_tiles):
                rows = slice(i * TILE, (i + 1) * TILE)
                for g in range(groups):
                    for s in range(KEEP):
                        src = src_ref[(i * groups + g) * KEEP + s]
                        cur = bzero
                        for t in range(GROUP):
                            col = (g * GROUP + t) * TILE
                            cur = jnp.where(src == t, o_ref[rows, col:col + TILE], cur)
                        out = (g * KEEP + s) * TILE
                        packed_ref[rows, out:out + TILE] = cur


def expand_group(dst, src_ref, sel_ref, sel_base, rows, src_group, dst_group):
    zero = jnp.zeros((TILE, TILE), src_ref.dtype)
    base = src_group * KEEP * TILE
    s0 = src_ref[rows, base:base + TILE]
    s1 = src_ref[rows, base + TILE:base + 2 * TILE]
    for t in range(GROUP):
        sel = sel_ref[sel_base + t]
        col = (dst_group * GROUP + t) * TILE
        dst[rows, col:col + TILE] = jnp.where(sel == 0, s0, jnp.where(sel == 1, s1, zero))


def product(packed_rows, panel_a, panel_b, gblk, rpos, rsel, csel, own, src, square=None):
    blocks, rows, _ = packed_rows.shape
    step_k = panel_a.shape[1]
    cols = 2 * GROUP * TILE
    k_tiles = blocks * step_k // TILE
    index = lambda s, g, p, r, c, o, q: (0, 0)
    in_specs = [
        pl.BlockSpec((None, rows, packed_rows.shape[2]), lambda s, g, p, r, c, o, q: (p[g[s]], 0, 0)),
        pl.BlockSpec((None, step_k, panel_a.shape[2]), lambda s, g, p, r, c, o, q: (s, 0, 0)),
        pl.BlockSpec((None, step_k, panel_b.shape[2]), lambda s, g, p, r, c, o, q: (s, 0, 0)),
    ]
    operands = [packed_rows, panel_a, panel_b]
    if square is None:
        out_shape = (jax.ShapeDtypeStruct((rows, cols), jnp.bfloat16),
                     jax.ShapeDtypeStruct((rows, cols * KEEP // GROUP), jnp.bfloat16))
        out_specs = (pl.BlockSpec((rows, cols), index), pl.BlockSpec((rows, cols * KEEP // GROUP), index))
    else:
        in_specs.append(pl.BlockSpec((rows, cols), index))
        operands.append(square)
        out_shape = jax.ShapeDtypeStruct((rows, cols), jnp.bfloat16)
        out_specs = pl.BlockSpec((rows, cols), index)
    return pl.pallas_call(
        functools.partial(product_kernel, k_tiles, square is None),
        out_shape=out_shape,
        grid_spec=pltpu.PrefetchScalarGridSpec(
            num_scalar_prefetch=6,
            grid=(blocks,),
            in_specs=in_specs,
            out_specs=out_specs,
            scratch_shapes=[
                pltpu.VMEM((rows, step_k), packed_rows.dtype),
                pltpu.VMEM((step_k, cols), panel_a.dtype),
                pltpu.VMEM((rows, cols), jnp.float32),
            ],
        ),
        compiler_params=pltpu.CompilerParams(dimension_semantics=("arbitrary",)),
        cost_estimate=pl.CostEstimate(
            flops=2 * rows * blocks * step_k * cols,
            transcendentals=0,
            bytes_accessed=2 * (packed_rows.size + panel_a.size + panel_b.size) + 4 * rows * cols,
        ),
    )(gblk, rpos, rsel, csel, own, src, *operands)


def ring_gather(x, axis, stride=1):
    size = lax.axis_size(axis)
    n = size // stride
    fwd_perm = [(i, (i + stride) % size) for i in range(size)]
    bwd_perm = [(i, (i - stride) % size) for i in range(size)]
    blocks = [None] * n
    blocks[0] = x
    if n == 4:
        far_perm = [(i, (i + 2 * stride) % size) for i in range(size)]
        blocks[1] = lax.ppermute(x, axis, bwd_perm)
        blocks[3] = lax.ppermute(x, axis, fwd_perm)
        blocks[2] = lax.ppermute(x, axis, far_perm)
        return blocks
    f, b = x, x
    half = n // 2
    for k in range(1, half):
        f = lax.ppermute(f, axis, fwd_perm)
        b = lax.ppermute(b, axis, bwd_perm)
        blocks[n - k] = f
        blocks[k] = b
    cut = x.shape[0] // 2
    top = lax.ppermute(f[:cut], axis, fwd_perm)
    bottom = lax.ppermute(b[cut:], axis, bwd_perm)
    blocks[half] = jnp.concatenate([top, bottom], axis=0)
    return blocks


def shards(density, pattern):
    row_count, col_width = density.shape
    layers = lax.axis_size("layer")
    cols_n = lax.axis_size("col")
    rows_n = lax.axis_size("row")
    c = lax.axis_index("col")
    l = lax.axis_index("layer")
    r = lax.axis_index("row")
    row_tile0 = (c * layers + l) * (row_count // TILE)
    col_tile0 = r * (col_width // TILE)
    live = pattern > 0
    own_rows = lax.dynamic_slice_in_dim(live, row_tile0, row_count // TILE, axis=0)
    own_cols = lax.dynamic_slice_in_dim(live, col_tile0, col_width // TILE, axis=1)
    own = lax.dynamic_slice_in_dim(own_rows, col_tile0, col_width // TILE, axis=1)

    groups = lambda m: m.reshape(m.shape[0], m.shape[1] // GROUP, GROUP)
    own_occ = groups(own)
    rsel = slot_of_tile(groups(own_rows)).reshape(-1)
    csel = slot_of_tile(groups(own_cols)).reshape(-1)

    packed = compress(density, own_occ)
    width = packed.shape[1] // 2
    part_a, part_b = packed[:, :width], packed[:, width:]
    along_col = jnp.stack(ring_gather(part_a, "col"))
    by_layer = jnp.roll(jnp.stack(ring_gather(along_col, "layer")), l, axis=0)
    panel_a = by_layer.transpose(1, 0, 2, 3).reshape(cols_n, layers * row_count, width)
    by_layer_b = jnp.roll(jnp.stack(ring_gather(part_b, "layer")), l, axis=0)
    piece_b = by_layer_b.reshape(layers * row_count, width)
    panel_b = jnp.stack(ring_gather(piece_b, "col"))

    steps = jnp.arange(cols_n, dtype=jnp.int32)
    gblk = (c + steps) % cols_n

    partner = [(i, i ^ 1) for i in range(rows_n)]
    half_n = rows_n // 2
    held = jnp.concatenate([(r + 2 * steps[:half_n]) % rows_n, ((r ^ 1) + 2 * steps[:half_n]) % rows_n])
    rpos = jnp.sum(jnp.where(held[None, :] == steps[:, None], steps[None, :], 0), axis=1).astype(jnp.int32)

    own_flat = own.astype(jnp.int32).reshape(-1)
    own_src = tile_of_slot(own_occ).reshape(-1)

    def gather_rows(packed):
        mine = jnp.stack(ring_gather(packed, "row", stride=2))
        theirs = lax.ppermute(mine, "row", partner)
        return jnp.concatenate([mine, theirs], axis=0)

    tables = (gblk, rpos, rsel, csel, own_flat, own_src)
    square, packed_square = product(gather_rows(packed), panel_a, panel_b, *tables)
    return product(gather_rows(packed_square), panel_a, panel_b, *tables, square=square)


def solution(mesh):
    return jax.shard_map(
        shards,
        mesh=mesh,
        in_specs=(P(("col", "layer"), "row"), P()),
        out_specs=P(("col", "layer"), "row"),
        check_vma=False,
    )
```

```python
import functools

import jax
import jax.numpy as jnp
from jax import lax
from jax.experimental import pallas as pl
from jax.experimental.pallas import tpu as pltpu
from jax.sharding import PartitionSpec as P

TILE = 128
GROUP = 4
KEEP = 2


def slot_of_tile(occ):
    count = occ.astype(jnp.int32)
    before = jnp.cumsum(count, axis=-1) - count
    return jnp.where(occ, before, KEEP).astype(jnp.int32)


def tile_of_slot(occ):
    slot = slot_of_tile(occ)
    tiles = jnp.arange(GROUP, dtype=jnp.int32)
    picks = [jnp.min(jnp.where(slot == s, tiles, GROUP), axis=-1) for s in range(KEEP)]
    return jnp.stack(picks, axis=-1).astype(jnp.int32)


def compress_kernel(src_ref, x_ref, o_ref):
    row_tiles = x_ref.shape[0] // TILE
    groups = x_ref.shape[1] // (GROUP * TILE)
    zero = jnp.zeros((TILE, TILE), x_ref.dtype)
    for i in range(row_tiles):
        rows = slice(i * TILE, (i + 1) * TILE)
        for g in range(groups):
            for s in range(KEEP):
                src = src_ref[(i * groups + g) * KEEP + s]
                cur = zero
                for t in range(GROUP):
                    col = (g * GROUP + t) * TILE
                    cur = jnp.where(src == t, x_ref[rows, col:col + TILE], cur)
                out = (g * KEEP + s) * TILE
                o_ref[rows, out:out + TILE] = cur


def compress(x, occ):
    rows, cols = x.shape
    src = tile_of_slot(occ).reshape(-1)
    return pl.pallas_call(
        compress_kernel,
        out_shape=jax.ShapeDtypeStruct((rows, cols * KEEP // GROUP), x.dtype),
        grid_spec=pltpu.PrefetchScalarGridSpec(
            num_scalar_prefetch=1,
            grid=(1,),
            in_specs=[pl.BlockSpec((rows, cols), lambda i, s: (0, 0))],
            out_specs=pl.BlockSpec((rows, cols * KEEP // GROUP), lambda i, s: (0, 0)),
        ),
    )(src, x)


def product_kernel(k_tiles, finish_square, gblk_ref, rpos_ref, rsel_ref, csel_ref, own_ref, src_ref, lay_ref,
                   rp_ref, cpa_ref,
                   cpb_ref, *rest):
    if finish_square:
        o_ref, packed_ref, rpx, cpx, acc = rest
    else:
        sq_ref, o_ref, rpx, cpx, acc = rest
    step = pl.program_id(0)
    step_tiles = cpb_ref.shape[0] // TILE
    layers = cpa_ref.shape[0]
    part_tiles = step_tiles // layers
    row_tiles = rp_ref.shape[0] // TILE
    col_tiles = o_ref.shape[1] // TILE
    block = gblk_ref[step]
    layer = lay_ref[0]

    def expand_panel_tile(kt, carry):
        rows = pl.ds(pl.multiple_of(kt * TILE, TILE), TILE)
        base = ((block * step_tiles + kt) * 2) * GROUP
        offset = (kt // part_tiles - layer + layers) % layers
        part_rows = pl.ds(pl.multiple_of((kt % part_tiles) * TILE, TILE), TILE)
        expand_group(cpx, cpa_ref.at[offset], csel_ref, base, part_rows, 0, 0, dst_rows=rows)
        expand_group(cpx, cpb_ref, csel_ref, base + GROUP, rows, 0, 1)
        return carry

    lax.fori_loop(0, step_tiles, expand_panel_tile, 0)
    for i in range(row_tiles):
        rows = slice(i * TILE, (i + 1) * TILE)
        for q in range(step_tiles // GROUP):
            expand_group(rpx, rp_ref, rsel_ref, i * k_tiles + block * step_tiles + q * GROUP, rows, q, q)

    @pl.when(step == 0)
    def _():
        acc[...] = jnp.zeros_like(acc)

    acc[...] += jnp.dot(rpx[...], cpx[...], preferred_element_type=jnp.float32)

    @pl.when(step == pl.num_programs(0) - 1)
    def _():
        zero = jnp.zeros((TILE, TILE), jnp.float32)
        for i in range(row_tiles):
            rows = slice(i * TILE, (i + 1) * TILE)
            for j in range(col_tiles):
                cols = slice(j * TILE, (j + 1) * TILE)
                masked = jnp.where(own_ref[i * col_tiles + j] > 0, acc[rows, cols], zero)
                if finish_square:
                    o_ref[rows, cols] = masked.astype(o_ref.dtype)
                else:
                    purified = 3.0 * sq_ref[rows, cols].astype(jnp.float32) - 2.0 * masked
                    o_ref[rows, cols] = purified.astype(o_ref.dtype)
        if finish_square:
            groups = col_tiles // GROUP
            bzero = jnp.zeros((TILE, TILE), o_ref.dtype)
            for i in range(row_tiles):
                rows = slice(i * TILE, (i + 1) * TILE)
                for g in range(groups):
                    for s in range(KEEP):
                        src = src_ref[(i * groups + g) * KEEP + s]
                        cur = bzero
                        for t in range(GROUP):
                            col = (g * GROUP + t) * TILE
                            cur = jnp.where(src == t, o_ref[rows, col:col + TILE], cur)
                        out = (g * KEEP + s) * TILE
                        packed_ref[rows, out:out + TILE] = cur


def expand_group(dst, src_ref, sel_ref, sel_base, rows, src_group, dst_group, dst_rows=None):
    dst_rows = rows if dst_rows is None else dst_rows
    zero = jnp.zeros((TILE, TILE), src_ref.dtype)
    base = src_group * KEEP * TILE
    s0 = src_ref[rows, base:base + TILE]
    s1 = src_ref[rows, base + TILE:base + 2 * TILE]
    for t in range(GROUP):
        sel = sel_ref[sel_base + t]
        col = (dst_group * GROUP + t) * TILE
        dst[dst_rows, col:col + TILE] = jnp.where(sel == 0, s0, jnp.where(sel == 1, s1, zero))


def product(packed_rows, panel_a, panel_b, gblk, rpos, rsel, csel, own, src, lay, square=None):
    blocks, rows, _ = packed_rows.shape
    step_k = panel_b.shape[1]
    cols = 2 * GROUP * TILE
    k_tiles = blocks * step_k // TILE
    index = lambda s, g, p, r, c, o, q, y: (0, 0)
    in_specs = [
        pl.BlockSpec((None, rows, packed_rows.shape[2]), lambda s, g, p, r, c, o, q, y: (p[g[s]], 0, 0)),
        pl.BlockSpec((panel_a.shape[0], None) + panel_a.shape[2:], lambda s, g, p, r, c, o, q, y: (0, s, 0, 0)),
        pl.BlockSpec((None, step_k, panel_b.shape[2]), lambda s, g, p, r, c, o, q, y: (s, 0, 0)),
    ]
    operands = [packed_rows, panel_a, panel_b]
    if square is None:
        out_shape = (jax.ShapeDtypeStruct((rows, cols), jnp.bfloat16),
                     jax.ShapeDtypeStruct((rows, cols * KEEP // GROUP), jnp.bfloat16))
        out_specs = (pl.BlockSpec((rows, cols), index), pl.BlockSpec((rows, cols * KEEP // GROUP), index))
    else:
        in_specs.append(pl.BlockSpec((rows, cols), index))
        operands.append(square)
        out_shape = jax.ShapeDtypeStruct((rows, cols), jnp.bfloat16)
        out_specs = pl.BlockSpec((rows, cols), index)
    return pl.pallas_call(
        functools.partial(product_kernel, k_tiles, square is None),
        out_shape=out_shape,
        grid_spec=pltpu.PrefetchScalarGridSpec(
            num_scalar_prefetch=7,
            grid=(blocks,),
            in_specs=in_specs,
            out_specs=out_specs,
            scratch_shapes=[
                pltpu.VMEM((rows, step_k), packed_rows.dtype),
                pltpu.VMEM((step_k, cols), panel_b.dtype),
                pltpu.VMEM((rows, cols), jnp.float32),
            ],
        ),
        compiler_params=pltpu.CompilerParams(dimension_semantics=("arbitrary",)),
        cost_estimate=pl.CostEstimate(
            flops=2 * rows * blocks * step_k * cols,
            transcendentals=0,
            bytes_accessed=2 * (packed_rows.size + panel_a.size + panel_b.size) + 4 * rows * cols,
        ),
    )(gblk, rpos, rsel, csel, own, src, lay, *operands)


def ring_gather(x, axis, stride=1):
    size = lax.axis_size(axis)
    n = size // stride
    fwd_perm = [(i, (i + stride) % size) for i in range(size)]
    bwd_perm = [(i, (i - stride) % size) for i in range(size)]
    blocks = [None] * n
    blocks[0] = x
    f, b = x, x
    half = n // 2
    for k in range(1, half):
        f = lax.ppermute(f, axis, fwd_perm)
        b = lax.ppermute(b, axis, bwd_perm)
        blocks[n - k] = f
        blocks[k] = b
    cut = x.shape[0] // 2
    top = lax.ppermute(f[:cut], axis, fwd_perm)
    bottom = lax.ppermute(b[cut:], axis, bwd_perm)
    blocks[half] = jnp.concatenate([top, bottom], axis=0)
    return blocks


def shards(density, pattern):
    row_count, col_width = density.shape
    layers = lax.axis_size("layer")
    cols_n = lax.axis_size("col")
    rows_n = lax.axis_size("row")
    c = lax.axis_index("col")
    l = lax.axis_index("layer")
    r = lax.axis_index("row")
    row_tile0 = (c * layers + l) * (row_count // TILE)
    col_tile0 = r * (col_width // TILE)
    live = pattern > 0
    own_rows = lax.dynamic_slice_in_dim(live, row_tile0, row_count // TILE, axis=0)
    own_cols = lax.dynamic_slice_in_dim(live, col_tile0, col_width // TILE, axis=1)
    own = lax.dynamic_slice_in_dim(own_rows, col_tile0, col_width // TILE, axis=1)

    groups = lambda m: m.reshape(m.shape[0], m.shape[1] // GROUP, GROUP)
    own_occ = groups(own)
    rsel = slot_of_tile(groups(own_rows)).reshape(-1)
    csel = slot_of_tile(groups(own_cols)).reshape(-1)

    packed = compress(density, own_occ)
    width = packed.shape[1] // 2
    part_a, part_b = packed[:, :width], packed[:, width:]
    along_col = jnp.stack(ring_gather(part_a, "col"))
    panel_a = jnp.stack(ring_gather(along_col, "layer"))
    by_layer_b = jnp.roll(jnp.stack(ring_gather(part_b, "layer")), l, axis=0)
    piece_b = by_layer_b.reshape(layers * row_count, width)
    panel_b = jnp.stack(ring_gather(piece_b, "col"))

    steps = jnp.arange(cols_n, dtype=jnp.int32)
    gblk = (c + steps) % cols_n

    partner = [(i, i ^ 1) for i in range(rows_n)]
    half_n = rows_n // 2
    held = jnp.concatenate([(r + 2 * steps[:half_n]) % rows_n, ((r ^ 1) + 2 * steps[:half_n]) % rows_n])
    rpos = jnp.sum(jnp.where(held[None, :] == steps[:, None], steps[None, :], 0), axis=1).astype(jnp.int32)

    own_flat = own.astype(jnp.int32).reshape(-1)
    own_src = tile_of_slot(own_occ).reshape(-1)

    def gather_rows(packed):
        mine = jnp.stack(ring_gather(packed, "row", stride=2))
        theirs = lax.ppermute(mine, "row", partner)
        return jnp.concatenate([mine, theirs], axis=0)

    tables = (gblk, rpos, rsel, csel, own_flat, own_src, jnp.full((1,), l, jnp.int32))
    square, packed_square = product(gather_rows(packed), panel_a, panel_b, *tables)
    return product(gather_rows(packed_square), panel_a, panel_b, *tables, square=square)


def solution(mesh):
    return jax.shard_map(
        shards,
        mesh=mesh,
        in_specs=(P(("col", "layer"), "row"), P()),
        out_specs=P(("col", "layer"), "row"),
        check_vma=False,
    )
```

```python
import functools

import jax
import jax.numpy as jnp
from jax import lax
from jax.experimental import pallas as pl
from jax.experimental.pallas import tpu as pltpu
from jax.sharding import PartitionSpec as P

TILE = 128
GROUP = 4
KEEP = 2
SMALL_BYTES = 1 << 18


def slot_of_tile(occ):
    count = occ.astype(jnp.int32)
    before = jnp.cumsum(count, axis=-1) - count
    return jnp.where(occ, before, KEEP).astype(jnp.int32)


def tile_of_slot(occ):
    slot = slot_of_tile(occ)
    tiles = jnp.arange(GROUP, dtype=jnp.int32)
    picks = [jnp.min(jnp.where(slot == s, tiles, GROUP), axis=-1) for s in range(KEEP)]
    return jnp.stack(picks, axis=-1).astype(jnp.int32)


def compress_kernel(src_ref, x_ref, o_ref):
    row_tiles = x_ref.shape[0] // TILE
    groups = x_ref.shape[1] // (GROUP * TILE)
    zero = jnp.zeros((TILE, TILE), x_ref.dtype)
    for i in range(row_tiles):
        rows = slice(i * TILE, (i + 1) * TILE)
        for g in range(groups):
            for s in range(KEEP):
                src = src_ref[(i * groups + g) * KEEP + s]
                cur = zero
                for t in range(GROUP):
                    col = (g * GROUP + t) * TILE
                    cur = jnp.where(src == t, x_ref[rows, col:col + TILE], cur)
                out = (g * KEEP + s) * TILE
                o_ref[rows, out:out + TILE] = cur


def compress(x, occ):
    rows, cols = x.shape
    src = tile_of_slot(occ).reshape(-1)
    return pl.pallas_call(
        compress_kernel,
        out_shape=jax.ShapeDtypeStruct((rows, cols * KEEP // GROUP), x.dtype),
        grid_spec=pltpu.PrefetchScalarGridSpec(
            num_scalar_prefetch=1,
            grid=(1,),
            in_specs=[pl.BlockSpec((rows, cols), lambda i, s: (0, 0))],
            out_specs=pl.BlockSpec((rows, cols * KEEP // GROUP), lambda i, s: (0, 0)),
        ),
    )(src, x)


def product_kernel(k_tiles, finish_square, gblk_ref, rpos_ref, rsel_ref, csel_ref, own_ref, src_ref, rp_ref, cpa_ref,
                   cpb_ref, *rest):
    if finish_square:
        o_ref, packed_ref, rpx, cpx, acc = rest
    else:
        sq_ref, o_ref, rpx, cpx, acc = rest
    step = pl.program_id(0)
    step_tiles = cpa_ref.shape[0] // TILE
    row_tiles = rp_ref.shape[0] // TILE
    col_tiles = o_ref.shape[1] // TILE
    block = gblk_ref[step]

    def expand_panel_tile(kt, carry):
        rows = pl.ds(pl.multiple_of(kt * TILE, TILE), TILE)
        for g, cp_ref in enumerate((cpa_ref, cpb_ref)):
            expand_group(cpx, cp_ref, csel_ref, ((block * step_tiles + kt) * 2 + g) * GROUP, rows, 0, g)
        return carry

    lax.fori_loop(0, step_tiles, expand_panel_tile, 0)
    for i in range(row_tiles):
        rows = slice(i * TILE, (i + 1) * TILE)
        for q in range(step_tiles // GROUP):
            expand_group(rpx, rp_ref, rsel_ref, i * k_tiles + block * step_tiles + q * GROUP, rows, q, q)

    @pl.when(step == 0)
    def _():
        acc[...] = jnp.zeros_like(acc)

    acc[...] += jnp.dot(rpx[...], cpx[...], preferred_element_type=jnp.float32)

    @pl.when(step == pl.num_programs(0) - 1)
    def _():
        zero = jnp.zeros((TILE, TILE), jnp.float32)
        for i in range(row_tiles):
            rows = slice(i * TILE, (i + 1) * TILE)
            for j in range(col_tiles):
                cols = slice(j * TILE, (j + 1) * TILE)
                masked = jnp.where(own_ref[i * col_tiles + j] > 0, acc[rows, cols], zero)
                if finish_square:
                    o_ref[rows, cols] = masked.astype(o_ref.dtype)
                else:
                    purified = 3.0 * sq_ref[rows, cols].astype(jnp.float32) - 2.0 * masked
                    o_ref[rows, cols] = purified.astype(o_ref.dtype)
        if finish_square:
            groups = col_tiles // GROUP
            bzero = jnp.zeros((TILE, TILE), o_ref.dtype)
            for i in range(row_tiles):
                rows = slice(i * TILE, (i + 1) * TILE)
                for g in range(groups):
                    for s in range(KEEP):
                        src = src_ref[(i * groups + g) * KEEP + s]
                        cur = bzero
                        for t in range(GROUP):
                            col = (g * GROUP + t) * TILE
                            cur = jnp.where(src == t, o_ref[rows, col:col + TILE], cur)
                        out = (g * KEEP + s) * TILE
                        packed_ref[rows, out:out + TILE] = cur


def expand_group(dst, src_ref, sel_ref, sel_base, rows, src_group, dst_group):
    zero = jnp.zeros((TILE, TILE), src_ref.dtype)
    base = src_group * KEEP * TILE
    s0 = src_ref[rows, base:base + TILE]
    s1 = src_ref[rows, base + TILE:base + 2 * TILE]
    for t in range(GROUP):
        sel = sel_ref[sel_base + t]
        col = (dst_group * GROUP + t) * TILE
        dst[rows, col:col + TILE] = jnp.where(sel == 0, s0, jnp.where(sel == 1, s1, zero))


def product(packed_rows, panel_a, panel_b, gblk, rpos, rsel, csel, own, src, square=None):
    blocks, rows, _ = packed_rows.shape
    step_k = panel_a.shape[1]
    cols = 2 * GROUP * TILE
    k_tiles = blocks * step_k // TILE
    index = lambda s, g, p, r, c, o, q: (0, 0)
    in_specs = [
        pl.BlockSpec((None, rows, packed_rows.shape[2]), lambda s, g, p, r, c, o, q: (p[g[s]], 0, 0)),
        pl.BlockSpec((None, step_k, panel_a.shape[2]), lambda s, g, p, r, c, o, q: (s, 0, 0)),
        pl.BlockSpec((None, step_k, panel_b.shape[2]), lambda s, g, p, r, c, o, q: (s, 0, 0)),
    ]
    operands = [packed_rows, panel_a, panel_b]
    if square is None:
        out_shape = (jax.ShapeDtypeStruct((rows, cols), jnp.bfloat16),
                     jax.ShapeDtypeStruct((rows, cols * KEEP // GROUP), jnp.bfloat16))
        out_specs = (pl.BlockSpec((rows, cols), index), pl.BlockSpec((rows, cols * KEEP // GROUP), index))
    else:
        in_specs.append(pl.BlockSpec((rows, cols), index))
        operands.append(square)
        out_shape = jax.ShapeDtypeStruct((rows, cols), jnp.bfloat16)
        out_specs = pl.BlockSpec((rows, cols), index)
    return pl.pallas_call(
        functools.partial(product_kernel, k_tiles, square is None),
        out_shape=out_shape,
        grid_spec=pltpu.PrefetchScalarGridSpec(
            num_scalar_prefetch=6,
            grid=(blocks,),
            in_specs=in_specs,
            out_specs=out_specs,
            scratch_shapes=[
                pltpu.VMEM((rows, step_k), packed_rows.dtype),
                pltpu.VMEM((step_k, cols), panel_a.dtype),
                pltpu.VMEM((rows, cols), jnp.float32),
            ],
        ),
        compiler_params=pltpu.CompilerParams(dimension_semantics=("arbitrary",)),
        cost_estimate=pl.CostEstimate(
            flops=2 * rows * blocks * step_k * cols,
            transcendentals=0,
            bytes_accessed=2 * (packed_rows.size + panel_a.size + panel_b.size) + 4 * rows * cols,
        ),
    )(gblk, rpos, rsel, csel, own, src, *operands)


def ring_gather(x, axis, stride=1):
    size = lax.axis_size(axis)
    n = size // stride
    fwd_perm = [(i, (i + stride) % size) for i in range(size)]
    bwd_perm = [(i, (i - stride) % size) for i in range(size)]
    blocks = [None] * n
    blocks[0] = x
    f, b = x, x
    half = n // 2
    for k in range(1, half):
        f = lax.ppermute(f, axis, fwd_perm)
        b = lax.ppermute(b, axis, bwd_perm)
        blocks[n - k] = f
        blocks[k] = b
    if x.size * x.dtype.itemsize <= SMALL_BYTES:
        blocks[half] = lax.ppermute(f, axis, fwd_perm)
        return blocks
    cut = x.shape[0] // 2
    top = lax.ppermute(f[:cut], axis, fwd_perm)
    bottom = lax.ppermute(b[cut:], axis, bwd_perm)
    blocks[half] = jnp.concatenate([top, bottom], axis=0)
    return blocks


def shards(density, pattern):
    row_count, col_width = density.shape
    layers = lax.axis_size("layer")
    cols_n = lax.axis_size("col")
    rows_n = lax.axis_size("row")
    c = lax.axis_index("col")
    l = lax.axis_index("layer")
    r = lax.axis_index("row")
    row_tile0 = (c * layers + l) * (row_count // TILE)
    col_tile0 = r * (col_width // TILE)
    live = pattern > 0
    own_rows = lax.dynamic_slice_in_dim(live, row_tile0, row_count // TILE, axis=0)
    own_cols = lax.dynamic_slice_in_dim(live, col_tile0, col_width // TILE, axis=1)
    own = lax.dynamic_slice_in_dim(own_rows, col_tile0, col_width // TILE, axis=1)

    groups = lambda m: m.reshape(m.shape[0], m.shape[1] // GROUP, GROUP)
    own_occ = groups(own)
    rsel = slot_of_tile(groups(own_rows)).reshape(-1)
    csel = slot_of_tile(groups(own_cols)).reshape(-1)

    packed = compress(density, own_occ)
    width = packed.shape[1] // 2
    part_a, part_b = packed[:, :width], packed[:, width:]
    along_col = jnp.stack(ring_gather(part_a, "col"))
    by_layer = jnp.roll(jnp.stack(ring_gather(along_col, "layer")), l, axis=0)
    panel_a = by_layer.transpose(1, 0, 2, 3).reshape(cols_n, layers * row_count, width)
    by_layer_b = jnp.roll(jnp.stack(ring_gather(part_b, "layer")), l, axis=0)
    piece_b = by_layer_b.reshape(layers * row_count, width)
    panel_b = jnp.stack(ring_gather(piece_b, "col"))

    steps = jnp.arange(cols_n, dtype=jnp.int32)
    gblk = (c + steps) % cols_n

    partner = [(i, i ^ 1) for i in range(rows_n)]
    half_n = rows_n // 2
    held = jnp.concatenate([(r + 2 * steps[:half_n]) % rows_n, ((r ^ 1) + 2 * steps[:half_n]) % rows_n])
    rpos = jnp.sum(jnp.where(held[None, :] == steps[:, None], steps[None, :], 0), axis=1).astype(jnp.int32)

    own_flat = own.astype(jnp.int32).reshape(-1)
    own_src = tile_of_slot(own_occ).reshape(-1)

    def gather_rows(packed):
        mine = jnp.stack(ring_gather(packed, "row", stride=2))
        theirs = lax.ppermute(mine, "row", partner)
        return jnp.concatenate([mine, theirs], axis=0)

    tables = (gblk, rpos, rsel, csel, own_flat, own_src)
    square, packed_square = product(gather_rows(packed), panel_a, panel_b, *tables)
    return product(gather_rows(packed_square), panel_a, panel_b, *tables, square=square)


def solution(mesh):
    return jax.shard_map(
        shards,
        mesh=mesh,
        in_specs=(P(("col", "layer"), "row"), P()),
        out_specs=P(("col", "layer"), "row"),
        check_vma=False,
    )
```

```python
import functools

import jax
import jax.numpy as jnp
from jax import lax
from jax.experimental import pallas as pl
from jax.experimental.pallas import tpu as pltpu
from jax.sharding import PartitionSpec as P

TILE = 128
GROUP = 4
KEEP = 2
SMALL_BYTES = 1 << 18


def slot_of_tile(occ):
    count = occ.astype(jnp.int32)
    before = jnp.cumsum(count, axis=-1) - count
    return jnp.where(occ, before, KEEP).astype(jnp.int32)


def tile_of_slot(occ):
    slot = slot_of_tile(occ)
    tiles = jnp.arange(GROUP, dtype=jnp.int32)
    picks = [jnp.min(jnp.where(slot == s, tiles, GROUP), axis=-1) for s in range(KEEP)]
    return jnp.stack(picks, axis=-1).astype(jnp.int32)


def compress_kernel(src_ref, x_ref, o_ref):
    groups = x_ref.shape[1] // (GROUP * TILE)
    zero = jnp.zeros((TILE, TILE), x_ref.dtype)
    i = pl.program_id(0)
    for g in range(groups):
        for s in range(KEEP):
            src = src_ref[(i * groups + g) * KEEP + s]
            cur = zero
            for t in range(GROUP):
                col = (g * GROUP + t) * TILE
                cur = jnp.where(src == t, x_ref[:, col:col + TILE], cur)
            out = (g * KEEP + s) * TILE
            o_ref[:, out:out + TILE] = cur


def compress(x, occ):
    rows, cols = x.shape
    src = tile_of_slot(occ).reshape(-1)
    return pl.pallas_call(
        compress_kernel,
        out_shape=jax.ShapeDtypeStruct((rows, cols * KEEP // GROUP), x.dtype),
        grid_spec=pltpu.PrefetchScalarGridSpec(
            num_scalar_prefetch=1,
            grid=(rows // TILE,),
            in_specs=[pl.BlockSpec((TILE, cols), lambda i, s: (i, 0))],
            out_specs=pl.BlockSpec((TILE, cols * KEEP // GROUP), lambda i, s: (i, 0)),
        ),
    )(src, x)


def product_kernel(k_tiles, finish_square, gblk_ref, rpos_ref, rsel_ref, csel_ref, own_ref, src_ref, rp_ref, cpa_ref,
                   cpb_ref, *rest):
    if finish_square:
        o_ref, packed_ref, rpx, cpx, acc = rest
    else:
        sq_ref, o_ref, rpx, cpx, acc = rest
    step = pl.program_id(0)
    step_tiles = cpa_ref.shape[0] // TILE
    row_tiles = rp_ref.shape[0] // TILE
    col_tiles = o_ref.shape[1] // TILE
    block = gblk_ref[step]

    def expand_panel_tile(kt, carry):
        rows = pl.ds(pl.multiple_of(kt * TILE, TILE), TILE)
        for g, cp_ref in enumerate((cpa_ref, cpb_ref)):
            expand_group(cpx, cp_ref, csel_ref, ((block * step_tiles + kt) * 2 + g) * GROUP, rows, 0, g)
        return carry

    lax.fori_loop(0, step_tiles, expand_panel_tile, 0)
    for i in range(row_tiles):
        rows = slice(i * TILE, (i + 1) * TILE)
        for q in range(step_tiles // GROUP):
            expand_group(rpx, rp_ref, rsel_ref, i * k_tiles + block * step_tiles + q * GROUP, rows, q, q)

    @pl.when(step == 0)
    def _():
        acc[...] = jnp.zeros_like(acc)

    acc[...] += jnp.dot(rpx[...], cpx[...], preferred_element_type=jnp.float32)

    @pl.when(step == pl.num_programs(0) - 1)
    def _():
        zero = jnp.zeros((TILE, TILE), jnp.float32)
        for i in range(row_tiles):
            rows = slice(i * TILE, (i + 1) * TILE)
            for j in range(col_tiles):
                cols = slice(j * TILE, (j + 1) * TILE)
                masked = jnp.where(own_ref[i * col_tiles + j] > 0, acc[rows, cols], zero)
                if finish_square:
                    o_ref[rows, cols] = masked.astype(o_ref.dtype)
                else:
                    purified = 3.0 * sq_ref[rows, cols].astype(jnp.float32) - 2.0 * masked
                    o_ref[rows, cols] = purified.astype(o_ref.dtype)
        if finish_square:
            groups = col_tiles // GROUP
            bzero = jnp.zeros((TILE, TILE), o_ref.dtype)
            for i in range(row_tiles):
                rows = slice(i * TILE, (i + 1) * TILE)
                for g in range(groups):
                    for s in range(KEEP):
                        src = src_ref[(i * groups + g) * KEEP + s]
                        cur = bzero
                        for t in range(GROUP):
                            col = (g * GROUP + t) * TILE
                            cur = jnp.where(src == t, o_ref[rows, col:col + TILE], cur)
                        out = (g * KEEP + s) * TILE
                        packed_ref[rows, out:out + TILE] = cur


def expand_group(dst, src_ref, sel_ref, sel_base, rows, src_group, dst_group):
    zero = jnp.zeros((TILE, TILE), src_ref.dtype)
    base = src_group * KEEP * TILE
    s0 = src_ref[rows, base:base + TILE]
    s1 = src_ref[rows, base + TILE:base + 2 * TILE]
    for t in range(GROUP):
        sel = sel_ref[sel_base + t]
        col = (dst_group * GROUP + t) * TILE
        dst[rows, col:col + TILE] = jnp.where(sel == 0, s0, jnp.where(sel == 1, s1, zero))


def product(packed_rows, panel_a, panel_b, gblk, rpos, rsel, csel, own, src, square=None):
    blocks, rows, _ = packed_rows.shape
    step_k = panel_a.shape[1]
    cols = 2 * GROUP * TILE
    k_tiles = blocks * step_k // TILE
    index = lambda s, g, p, r, c, o, q: (0, 0)
    in_specs = [
        pl.BlockSpec((None, rows, packed_rows.shape[2]), lambda s, g, p, r, c, o, q: (p[g[s]], 0, 0)),
        pl.BlockSpec((None, step_k, panel_a.shape[2]), lambda s, g, p, r, c, o, q: (s, 0, 0)),
        pl.BlockSpec((None, step_k, panel_b.shape[2]), lambda s, g, p, r, c, o, q: (s, 0, 0)),
    ]
    operands = [packed_rows, panel_a, panel_b]
    if square is None:
        out_shape = (jax.ShapeDtypeStruct((rows, cols), jnp.bfloat16),
                     jax.ShapeDtypeStruct((rows, cols * KEEP // GROUP), jnp.bfloat16))
        out_specs = (pl.BlockSpec((rows, cols), index), pl.BlockSpec((rows, cols * KEEP // GROUP), index))
    else:
        in_specs.append(pl.BlockSpec((rows, cols), index))
        operands.append(square)
        out_shape = jax.ShapeDtypeStruct((rows, cols), jnp.bfloat16)
        out_specs = pl.BlockSpec((rows, cols), index)
    return pl.pallas_call(
        functools.partial(product_kernel, k_tiles, square is None),
        out_shape=out_shape,
        grid_spec=pltpu.PrefetchScalarGridSpec(
            num_scalar_prefetch=6,
            grid=(blocks,),
            in_specs=in_specs,
            out_specs=out_specs,
            scratch_shapes=[
                pltpu.VMEM((rows, step_k), packed_rows.dtype),
                pltpu.VMEM((step_k, cols), panel_a.dtype),
                pltpu.VMEM((rows, cols), jnp.float32),
            ],
        ),
        compiler_params=pltpu.CompilerParams(dimension_semantics=("arbitrary",)),
        cost_estimate=pl.CostEstimate(
            flops=2 * rows * blocks * step_k * cols,
            transcendentals=0,
            bytes_accessed=2 * (packed_rows.size + panel_a.size + panel_b.size) + 4 * rows * cols,
        ),
    )(gblk, rpos, rsel, csel, own, src, *operands)


def ring_gather(x, axis, stride=1):
    size = lax.axis_size(axis)
    n = size // stride
    fwd_perm = [(i, (i + stride) % size) for i in range(size)]
    bwd_perm = [(i, (i - stride) % size) for i in range(size)]
    blocks = [None] * n
    blocks[0] = x
    f, b = x, x
    half = n // 2
    for k in range(1, half):
        f = lax.ppermute(f, axis, fwd_perm)
        b = lax.ppermute(b, axis, bwd_perm)
        blocks[n - k] = f
        blocks[k] = b
    if x.size * x.dtype.itemsize <= SMALL_BYTES:
        blocks[half] = lax.ppermute(f, axis, fwd_perm)
        return blocks
    cut = x.shape[0] // 2
    top = lax.ppermute(f[:cut], axis, fwd_perm)
    bottom = lax.ppermute(b[cut:], axis, bwd_perm)
    blocks[half] = jnp.concatenate([top, bottom], axis=0)
    return blocks


def shards(density, pattern):
    row_count, col_width = density.shape
    layers = lax.axis_size("layer")
    cols_n = lax.axis_size("col")
    rows_n = lax.axis_size("row")
    c = lax.axis_index("col")
    l = lax.axis_index("layer")
    r = lax.axis_index("row")
    row_tile0 = (c * layers + l) * (row_count // TILE)
    col_tile0 = r * (col_width // TILE)
    live = pattern > 0
    own_rows = lax.dynamic_slice_in_dim(live, row_tile0, row_count // TILE, axis=0)
    own_cols = lax.dynamic_slice_in_dim(live, col_tile0, col_width // TILE, axis=1)
    own = lax.dynamic_slice_in_dim(own_rows, col_tile0, col_width // TILE, axis=1)

    groups = lambda m: m.reshape(m.shape[0], m.shape[1] // GROUP, GROUP)
    own_occ = groups(own)
    rsel = slot_of_tile(groups(own_rows)).reshape(-1)
    csel = slot_of_tile(groups(own_cols)).reshape(-1)

    packed = compress(density, own_occ)
    width = packed.shape[1] // 2
    part_a, part_b = packed[:, :width], packed[:, width:]
    along_col = jnp.stack(ring_gather(part_a, "col"))
    by_layer = jnp.roll(jnp.stack(ring_gather(along_col, "layer")), l, axis=0)
    panel_a = by_layer.transpose(1, 0, 2, 3).reshape(cols_n, layers * row_count, width)
    by_layer_b = jnp.roll(jnp.stack(ring_gather(part_b, "layer")), l, axis=0)
    piece_b = by_layer_b.reshape(layers * row_count, width)
    panel_b = jnp.stack(ring_gather(piece_b, "col"))

    steps = jnp.arange(cols_n, dtype=jnp.int32)
    gblk = (c + steps) % cols_n

    partner = [(i, i ^ 1) for i in range(rows_n)]
    half_n = rows_n // 2
    held = jnp.concatenate([(r + 2 * steps[:half_n]) % rows_n, ((r ^ 1) + 2 * steps[:half_n]) % rows_n])
    rpos = jnp.sum(jnp.where(held[None, :] == steps[:, None], steps[None, :], 0), axis=1).astype(jnp.int32)

    own_flat = own.astype(jnp.int32).reshape(-1)
    own_src = tile_of_slot(own_occ).reshape(-1)

    def gather_rows(packed):
        mine = jnp.stack(ring_gather(packed, "row", stride=2))
        theirs = lax.ppermute(mine, "row", partner)
        return jnp.concatenate([mine, theirs], axis=0)

    tables = (gblk, rpos, rsel, csel, own_flat, own_src)
    square, packed_square = product(gather_rows(packed), panel_a, panel_b, *tables)
    return product(gather_rows(packed_square), panel_a, panel_b, *tables, square=square)


def solution(mesh):
    return jax.shard_map(
        shards,
        mesh=mesh,
        in_specs=(P(("col", "layer"), "row"), P()),
        out_specs=P(("col", "layer"), "row"),
        check_vma=False,
    )
```

```python
import functools

import jax
import jax.numpy as jnp
from jax import lax
from jax.experimental import pallas as pl
from jax.experimental.pallas import tpu as pltpu
from jax.sharding import PartitionSpec as P

TILE = 128
GROUP = 4
KEEP = 2
SMALL_BYTES = 1 << 18


def slot_of_tile(occ):
    count = occ.astype(jnp.int32)
    before = jnp.cumsum(count, axis=-1) - count
    return jnp.where(occ, before, KEEP).astype(jnp.int32)


def tile_of_slot(occ):
    slot = slot_of_tile(occ)
    tiles = jnp.arange(GROUP, dtype=jnp.int32)
    picks = [jnp.min(jnp.where(slot == s, tiles, GROUP), axis=-1) for s in range(KEEP)]
    return jnp.stack(picks, axis=-1).astype(jnp.int32)


def compress_kernel(src_ref, x_ref, o_ref):
    groups = x_ref.shape[1] // (GROUP * TILE)
    zero = jnp.zeros((TILE, TILE), x_ref.dtype)
    i = pl.program_id(0)
    for g in range(groups):
        for s in range(KEEP):
            src = src_ref[(i * groups + g) * KEEP + s]
            cur = zero
            for t in range(GROUP):
                col = (g * GROUP + t) * TILE
                cur = jnp.where(src == t, x_ref[:, col:col + TILE], cur)
            out = (g * KEEP + s) * TILE
            o_ref[:, out:out + TILE] = cur


def compress(x, occ):
    rows, cols = x.shape
    src = tile_of_slot(occ).reshape(-1)
    return pl.pallas_call(
        compress_kernel,
        out_shape=jax.ShapeDtypeStruct((rows, cols * KEEP // GROUP), x.dtype),
        grid_spec=pltpu.PrefetchScalarGridSpec(
            num_scalar_prefetch=1,
            grid=(rows // TILE,),
            in_specs=[pl.BlockSpec((TILE, cols), lambda i, s: (i, 0))],
            out_specs=pl.BlockSpec((TILE, cols * KEEP // GROUP), lambda i, s: (i, 0)),
        ),
    )(src, x)


def product_kernel(k_tiles, finish_square, gblk_ref, rpos_ref, rsel_ref, csel_ref, own_ref, src_ref, rp_ref, cpa_ref,
                   cpb_ref, *rest):
    if finish_square:
        o_ref, packed_ref, rpx, cpx, acc = rest
    else:
        sq_ref, o_ref, rpx, cpx, acc = rest
    step = pl.program_id(0)
    step_tiles = cpa_ref.shape[0] // TILE
    row_tiles = rp_ref.shape[0] // TILE
    col_tiles = o_ref.shape[1] // TILE
    block = gblk_ref[step]

    def expand_panel_tile(kt, carry):
        rows = pl.ds(pl.multiple_of(kt * TILE, TILE), TILE)
        for g, cp_ref in enumerate((cpa_ref, cpb_ref)):
            expand_group(cpx, cp_ref, csel_ref, ((block * step_tiles + kt) * 2 + g) * GROUP, rows, 0, g)
        return carry

    lax.fori_loop(0, step_tiles, expand_panel_tile, 0)
    for i in range(row_tiles):
        rows = slice(i * TILE, (i + 1) * TILE)
        for q in range(step_tiles // GROUP):
            expand_group(rpx, rp_ref, rsel_ref, i * k_tiles + block * step_tiles + q * GROUP, rows, q, q)

    @pl.when(step == 0)
    def _():
        acc[...] = jnp.zeros_like(acc)

    acc[...] += jnp.dot(rpx[...], cpx[...], preferred_element_type=jnp.float32)

    @pl.when(step == pl.num_programs(0) - 1)
    def _():
        zero = jnp.zeros((TILE, TILE), jnp.float32)
        for i in range(row_tiles):
            rows = slice(i * TILE, (i + 1) * TILE)
            for j in range(col_tiles):
                cols = slice(j * TILE, (j + 1) * TILE)
                masked = jnp.where(own_ref[i * col_tiles + j] > 0, acc[rows, cols], zero)
                if finish_square:
                    o_ref[rows, cols] = masked.astype(o_ref.dtype)
                else:
                    purified = 3.0 * sq_ref[rows, cols].astype(jnp.float32) - 2.0 * masked
                    o_ref[rows, cols] = purified.astype(o_ref.dtype)
        if finish_square:
            groups = col_tiles // GROUP
            bzero = jnp.zeros((TILE, TILE), o_ref.dtype)
            for i in range(row_tiles):
                rows = slice(i * TILE, (i + 1) * TILE)
                for g in range(groups):
                    for s in range(KEEP):
                        src = src_ref[(i * groups + g) * KEEP + s]
                        cur = bzero
                        for t in range(GROUP):
                            col = (g * GROUP + t) * TILE
                            cur = jnp.where(src == t, o_ref[rows, col:col + TILE], cur)
                        out = (g * KEEP + s) * TILE
                        packed_ref[rows, out:out + TILE] = cur


def expand_group(dst, src_ref, sel_ref, sel_base, rows, src_group, dst_group):
    zero = jnp.zeros((TILE, TILE), src_ref.dtype)
    base = src_group * KEEP * TILE
    s0 = src_ref[rows, base:base + TILE]
    s1 = src_ref[rows, base + TILE:base + 2 * TILE]
    for t in range(GROUP):
        sel = sel_ref[sel_base + t]
        col = (dst_group * GROUP + t) * TILE
        dst[rows, col:col + TILE] = jnp.where(sel == 0, s0, jnp.where(sel == 1, s1, zero))


def product(packed_rows, panel_a, panel_b, gblk, rpos, rsel, csel, own, src, square=None):
    blocks, rows, _ = packed_rows.shape
    step_k = panel_a.shape[1]
    cols = 2 * GROUP * TILE
    k_tiles = blocks * step_k // TILE
    index = lambda s, g, p, r, c, o, q: (0, 0)
    in_specs = [
        pl.BlockSpec((None, rows, packed_rows.shape[2]), lambda s, g, p, r, c, o, q: (p[g[s]], 0, 0)),
        pl.BlockSpec((None, step_k, panel_a.shape[2]), lambda s, g, p, r, c, o, q: (s, 0, 0)),
        pl.BlockSpec((None, step_k, panel_b.shape[2]), lambda s, g, p, r, c, o, q: (s, 0, 0)),
    ]
    operands = [packed_rows, panel_a, panel_b]
    if square is None:
        out_shape = (jax.ShapeDtypeStruct((rows, cols), jnp.bfloat16),
                     jax.ShapeDtypeStruct((rows, cols * KEEP // GROUP), jnp.bfloat16))
        out_specs = (pl.BlockSpec((rows, cols), index), pl.BlockSpec((rows, cols * KEEP // GROUP), index))
    else:
        in_specs.append(pl.BlockSpec((rows, cols), index))
        operands.append(square)
        out_shape = jax.ShapeDtypeStruct((rows, cols), jnp.bfloat16)
        out_specs = pl.BlockSpec((rows, cols), index)
    return pl.pallas_call(
        functools.partial(product_kernel, k_tiles, square is None),
        out_shape=out_shape,
        grid_spec=pltpu.PrefetchScalarGridSpec(
            num_scalar_prefetch=6,
            grid=(blocks,),
            in_specs=in_specs,
            out_specs=out_specs,
            scratch_shapes=[
                pltpu.VMEM((rows, step_k), packed_rows.dtype),
                pltpu.VMEM((step_k, cols), panel_a.dtype),
                pltpu.VMEM((rows, cols), jnp.float32),
            ],
        ),
        compiler_params=pltpu.CompilerParams(dimension_semantics=("arbitrary",)),
        cost_estimate=pl.CostEstimate(
            flops=2 * rows * blocks * step_k * cols,
            transcendentals=0,
            bytes_accessed=2 * (packed_rows.size + panel_a.size + panel_b.size) + 4 * rows * cols,
        ),
    )(gblk, rpos, rsel, csel, own, src, *operands)


def ring_gather(x, axis, stride=1):
    size = lax.axis_size(axis)
    n = size // stride
    fwd_perm = [(i, (i + stride) % size) for i in range(size)]
    bwd_perm = [(i, (i - stride) % size) for i in range(size)]
    blocks = [None] * n
    blocks[0] = x
    f, b = x, x
    half = n // 2
    for k in range(1, half):
        f = lax.ppermute(f, axis, fwd_perm)
        b = lax.ppermute(b, axis, bwd_perm)
        blocks[n - k] = f
        blocks[k] = b
    if x.size * x.dtype.itemsize <= SMALL_BYTES:
        blocks[half] = lax.ppermute(f, axis, fwd_perm)
        return blocks
    cut = x.shape[0] // 2
    top = lax.ppermute(f[:cut], axis, fwd_perm)
    bottom = lax.ppermute(b[cut:], axis, bwd_perm)
    blocks[half] = jnp.concatenate([top, bottom], axis=0)
    return blocks


def shards(density, pattern):
    row_count, col_width = density.shape
    layers = lax.axis_size("layer")
    cols_n = lax.axis_size("col")
    rows_n = lax.axis_size("row")
    c = lax.axis_index("col")
    l = lax.axis_index("layer")
    r = lax.axis_index("row")
    row_tile0 = (c * layers + l) * (row_count // TILE)
    col_tile0 = r * (col_width // TILE)
    live = pattern > 0
    own_rows = lax.dynamic_slice_in_dim(live, row_tile0, row_count // TILE, axis=0)
    own_cols = lax.dynamic_slice_in_dim(live, col_tile0, col_width // TILE, axis=1)
    own = lax.dynamic_slice_in_dim(own_rows, col_tile0, col_width // TILE, axis=1)

    groups = lambda m: m.reshape(m.shape[0], m.shape[1] // GROUP, GROUP)
    own_occ = groups(own)
    rsel = slot_of_tile(groups(own_rows)).reshape(-1)
    csel = slot_of_tile(groups(own_cols)).reshape(-1)

    packed = compress(density, own_occ)
    width = packed.shape[1] // 2
    part_a, part_b = packed[:, :width], packed[:, width:]
    along_col = jnp.stack(ring_gather(part_a, "col"))
    by_layer = jnp.roll(jnp.stack(ring_gather(along_col, "layer")), l, axis=0)
    panel_a = by_layer.transpose(1, 0, 2, 3).reshape(cols_n, layers * row_count, width)
    by_layer_b = jnp.roll(jnp.stack(ring_gather(part_b, "layer")), l, axis=0)
    piece_b = by_layer_b.reshape(layers * row_count, width)
    panel_b = jnp.stack(ring_gather(piece_b, "col"))

    steps = jnp.arange(cols_n, dtype=jnp.int32)
    gblk = (c + steps) % cols_n

    partner = [(i, i ^ 1) for i in range(rows_n)]
    half_n = rows_n // 2
    held = jnp.concatenate([(r + 2 * steps[:half_n]) % rows_n, ((r ^ 1) + 2 * steps[:half_n]) % rows_n])
    rpos = jnp.sum(jnp.where(held[None, :] == steps[:, None], steps[None, :], 0), axis=1).astype(jnp.int32)

    own_flat = own.astype(jnp.int32).reshape(-1)
    own_src = tile_of_slot(own_occ).reshape(-1)

    def gather_rows(packed):
        mine = ring_gather(packed, "row", stride=2)
        theirs = [lax.ppermute(block, "row", partner) for block in mine]
        return jnp.stack(mine + theirs)

    tables = (gblk, rpos, rsel, csel, own_flat, own_src)
    square, packed_square = product(gather_rows(packed), panel_a, panel_b, *tables)
    return product(gather_rows(packed_square), panel_a, panel_b, *tables, square=square)


def solution(mesh):
    return jax.shard_map(
        shards,
        mesh=mesh,
        in_specs=(P(("col", "layer"), "row"), P()),
        out_specs=P(("col", "layer"), "row"),
        check_vma=False,
    )
```

```python
import functools

import jax
import jax.numpy as jnp
from jax import lax
from jax.experimental import pallas as pl
from jax.experimental.pallas import tpu as pltpu
from jax.sharding import PartitionSpec as P

TILE = 128
GROUP = 4
KEEP = 2
SMALL_BYTES = 1 << 17


def slot_of_tile(occ):
    count = occ.astype(jnp.int32)
    before = jnp.cumsum(count, axis=-1) - count
    return jnp.where(occ, before, KEEP).astype(jnp.int32)


def tile_of_slot(occ):
    slot = slot_of_tile(occ)
    tiles = jnp.arange(GROUP, dtype=jnp.int32)
    picks = [jnp.min(jnp.where(slot == s, tiles, GROUP), axis=-1) for s in range(KEEP)]
    return jnp.stack(picks, axis=-1).astype(jnp.int32)


def compress_kernel(src_ref, x_ref, o_ref):
    groups = x_ref.shape[1] // (GROUP * TILE)
    zero = jnp.zeros((TILE, TILE), x_ref.dtype)
    i = pl.program_id(0)
    for g in range(groups):
        for s in range(KEEP):
            src = src_ref[(i * groups + g) * KEEP + s]
            cur = zero
            for t in range(GROUP):
                col = (g * GROUP + t) * TILE
                cur = jnp.where(src == t, x_ref[:, col:col + TILE], cur)
            out = (g * KEEP + s) * TILE
            o_ref[:, out:out + TILE] = cur


def compress(x, occ):
    rows, cols = x.shape
    src = tile_of_slot(occ).reshape(-1)
    return pl.pallas_call(
        compress_kernel,
        out_shape=jax.ShapeDtypeStruct((rows, cols * KEEP // GROUP), x.dtype),
        grid_spec=pltpu.PrefetchScalarGridSpec(
            num_scalar_prefetch=1,
            grid=(rows // TILE,),
            in_specs=[pl.BlockSpec((TILE, cols), lambda i, s: (i, 0))],
            out_specs=pl.BlockSpec((TILE, cols * KEEP // GROUP), lambda i, s: (i, 0)),
        ),
    )(src, x)


def product_kernel(k_tiles, finish_square, gblk_ref, rpos_ref, rsel_ref, csel_ref, own_ref, src_ref, rp_ref, cpa_ref,
                   cpb_ref, *rest):
    if finish_square:
        o_ref, packed_ref, rpx, cpx, acc = rest
    else:
        sq_ref, o_ref, rpx, cpx, acc = rest
    step = pl.program_id(0)
    step_tiles = cpa_ref.shape[0] // TILE
    row_tiles = rp_ref.shape[0] // TILE
    col_tiles = o_ref.shape[1] // TILE
    block = gblk_ref[step]

    def expand_panel_tile(kt, carry):
        rows = pl.ds(pl.multiple_of(kt * TILE, TILE), TILE)
        for g, cp_ref in enumerate((cpa_ref, cpb_ref)):
            expand_group(cpx, cp_ref, csel_ref, ((block * step_tiles + kt) * 2 + g) * GROUP, rows, 0, g)
        return carry

    lax.fori_loop(0, step_tiles, expand_panel_tile, 0)
    for i in range(row_tiles):
        rows = slice(i * TILE, (i + 1) * TILE)
        for q in range(step_tiles // GROUP):
            expand_group(rpx, rp_ref, rsel_ref, i * k_tiles + block * step_tiles + q * GROUP, rows, q, q)

    @pl.when(step == 0)
    def _():
        acc[...] = jnp.zeros_like(acc)

    acc[...] += jnp.dot(rpx[...], cpx[...], preferred_element_type=jnp.float32)

    @pl.when(step == pl.num_programs(0) - 1)
    def _():
        zero = jnp.zeros((TILE, TILE), jnp.float32)
        for i in range(row_tiles):
            rows = slice(i * TILE, (i + 1) * TILE)
            for j in range(col_tiles):
                cols = slice(j * TILE, (j + 1) * TILE)
                masked = jnp.where(own_ref[i * col_tiles + j] > 0, acc[rows, cols], zero)
                if finish_square:
                    o_ref[rows, cols] = masked.astype(o_ref.dtype)
                else:
                    purified = 3.0 * sq_ref[rows, cols].astype(jnp.float32) - 2.0 * masked
                    o_ref[rows, cols] = purified.astype(o_ref.dtype)
        if finish_square:
            groups = col_tiles // GROUP
            bzero = jnp.zeros((TILE, TILE), o_ref.dtype)
            for i in range(row_tiles):
                rows = slice(i * TILE, (i + 1) * TILE)
                for g in range(groups):
                    for s in range(KEEP):
                        src = src_ref[(i * groups + g) * KEEP + s]
                        cur = bzero
                        for t in range(GROUP):
                            col = (g * GROUP + t) * TILE
                            cur = jnp.where(src == t, o_ref[rows, col:col + TILE], cur)
                        out = (g * KEEP + s) * TILE
                        packed_ref[rows, out:out + TILE] = cur


def expand_group(dst, src_ref, sel_ref, sel_base, rows, src_group, dst_group):
    zero = jnp.zeros((TILE, TILE), src_ref.dtype)
    base = src_group * KEEP * TILE
    s0 = src_ref[rows, base:base + TILE]
    s1 = src_ref[rows, base + TILE:base + 2 * TILE]
    for t in range(GROUP):
        sel = sel_ref[sel_base + t]
        col = (dst_group * GROUP + t) * TILE
        dst[rows, col:col + TILE] = jnp.where(sel == 0, s0, jnp.where(sel == 1, s1, zero))


def product(packed_rows, panel_a, panel_b, gblk, rpos, rsel, csel, own, src, square=None):
    blocks, rows, _ = packed_rows.shape
    step_k = panel_a.shape[1]
    cols = 2 * GROUP * TILE
    k_tiles = blocks * step_k // TILE
    index = lambda s, g, p, r, c, o, q: (0, 0)
    in_specs = [
        pl.BlockSpec((None, rows, packed_rows.shape[2]), lambda s, g, p, r, c, o, q: (p[g[s]], 0, 0)),
        pl.BlockSpec((None, step_k, panel_a.shape[2]), lambda s, g, p, r, c, o, q: (s, 0, 0)),
        pl.BlockSpec((None, step_k, panel_b.shape[2]), lambda s, g, p, r, c, o, q: (s, 0, 0)),
    ]
    operands = [packed_rows, panel_a, panel_b]
    if square is None:
        out_shape = (jax.ShapeDtypeStruct((rows, cols), jnp.bfloat16),
                     jax.ShapeDtypeStruct((rows, cols * KEEP // GROUP), jnp.bfloat16))
        out_specs = (pl.BlockSpec((rows, cols), index), pl.BlockSpec((rows, cols * KEEP // GROUP), index))
    else:
        in_specs.append(pl.BlockSpec((rows, cols), index))
        operands.append(square)
        out_shape = jax.ShapeDtypeStruct((rows, cols), jnp.bfloat16)
        out_specs = pl.BlockSpec((rows, cols), index)
    return pl.pallas_call(
        functools.partial(product_kernel, k_tiles, square is None),
        out_shape=out_shape,
        grid_spec=pltpu.PrefetchScalarGridSpec(
            num_scalar_prefetch=6,
            grid=(blocks,),
            in_specs=in_specs,
            out_specs=out_specs,
            scratch_shapes=[
                pltpu.VMEM((rows, step_k), packed_rows.dtype),
                pltpu.VMEM((step_k, cols), panel_a.dtype),
                pltpu.VMEM((rows, cols), jnp.float32),
            ],
        ),
        compiler_params=pltpu.CompilerParams(dimension_semantics=("arbitrary",)),
        cost_estimate=pl.CostEstimate(
            flops=2 * rows * blocks * step_k * cols,
            transcendentals=0,
            bytes_accessed=2 * (packed_rows.size + panel_a.size + panel_b.size) + 4 * rows * cols,
        ),
    )(gblk, rpos, rsel, csel, own, src, *operands)


def ring_gather(x, axis, stride=1):
    size = lax.axis_size(axis)
    n = size // stride
    fwd_perm = [(i, (i + stride) % size) for i in range(size)]
    bwd_perm = [(i, (i - stride) % size) for i in range(size)]
    blocks = [None] * n
    blocks[0] = x
    f, b = x, x
    half = n // 2
    for k in range(1, half):
        f = lax.ppermute(f, axis, fwd_perm)
        b = lax.ppermute(b, axis, bwd_perm)
        blocks[n - k] = f
        blocks[k] = b
    if x.size * x.dtype.itemsize <= SMALL_BYTES:
        blocks[half] = lax.ppermute(f, axis, fwd_perm)
        return blocks
    cut = x.shape[0] // 2
    top = lax.ppermute(f[:cut], axis, fwd_perm)
    bottom = lax.ppermute(b[cut:], axis, bwd_perm)
    blocks[half] = jnp.concatenate([top, bottom], axis=0)
    return blocks


def shards(density, pattern):
    row_count, col_width = density.shape
    layers = lax.axis_size("layer")
    cols_n = lax.axis_size("col")
    rows_n = lax.axis_size("row")
    c = lax.axis_index("col")
    l = lax.axis_index("layer")
    r = lax.axis_index("row")
    row_tile0 = (c * layers + l) * (row_count // TILE)
    col_tile0 = r * (col_width // TILE)
    live = pattern > 0
    own_rows = lax.dynamic_slice_in_dim(live, row_tile0, row_count // TILE, axis=0)
    own_cols = lax.dynamic_slice_in_dim(live, col_tile0, col_width // TILE, axis=1)
    own = lax.dynamic_slice_in_dim(own_rows, col_tile0, col_width // TILE, axis=1)

    groups = lambda m: m.reshape(m.shape[0], m.shape[1] // GROUP, GROUP)
    own_occ = groups(own)
    rsel = slot_of_tile(groups(own_rows)).reshape(-1)
    csel = slot_of_tile(groups(own_cols)).reshape(-1)

    packed = compress(density, own_occ)
    width = packed.shape[1] // 2
    part_a, part_b = packed[:, :width], packed[:, width:]
    along_col = jnp.stack(ring_gather(part_a, "col"))
    by_layer = jnp.roll(jnp.stack(ring_gather(along_col, "layer")), l, axis=0)
    panel_a = by_layer.transpose(1, 0, 2, 3).reshape(cols_n, layers * row_count, width)
    by_layer_b = jnp.roll(jnp.stack(ring_gather(part_b, "layer")), l, axis=0)
    piece_b = by_layer_b.reshape(layers * row_count, width)
    panel_b = jnp.stack(ring_gather(piece_b, "col"))

    steps = jnp.arange(cols_n, dtype=jnp.int32)
    gblk = (c + steps) % cols_n

    partner = [(i, i ^ 1) for i in range(rows_n)]
    half_n = rows_n // 2
    held = jnp.concatenate([(r + 2 * steps[:half_n]) % rows_n, ((r ^ 1) + 2 * steps[:half_n]) % rows_n])
    rpos = jnp.sum(jnp.where(held[None, :] == steps[:, None], steps[None, :], 0), axis=1).astype(jnp.int32)

    own_flat = own.astype(jnp.int32).reshape(-1)
    own_src = tile_of_slot(own_occ).reshape(-1)

    def gather_rows(packed):
        mine = jnp.stack(ring_gather(packed, "row", stride=2))
        theirs = lax.ppermute(mine, "row", partner)
        return jnp.concatenate([mine, theirs], axis=0)

    tables = (gblk, rpos, rsel, csel, own_flat, own_src)
    square, packed_square = product(gather_rows(packed), panel_a, panel_b, *tables)
    return product(gather_rows(packed_square), panel_a, panel_b, *tables, square=square)


def solution(mesh):
    return jax.shard_map(
        shards,
        mesh=mesh,
        in_specs=(P(("col", "layer"), "row"), P()),
        out_specs=P(("col", "layer"), "row"),
        check_vma=False,
    )
```

```python
import functools

import jax
import jax.numpy as jnp
from jax import lax
from jax.experimental import pallas as pl
from jax.experimental.pallas import tpu as pltpu
from jax.sharding import PartitionSpec as P

TILE = 128
GROUP = 4
KEEP = 2
SMALL_BYTES = 1 << 17


def slot_of_tile(occ):
    count = occ.astype(jnp.int32)
    before = jnp.cumsum(count, axis=-1) - count
    return jnp.where(occ, before, KEEP).astype(jnp.int32)


def tile_of_slot(occ):
    slot = slot_of_tile(occ)
    tiles = jnp.arange(GROUP, dtype=jnp.int32)
    picks = [jnp.min(jnp.where(slot == s, tiles, GROUP), axis=-1) for s in range(KEEP)]
    return jnp.stack(picks, axis=-1).astype(jnp.int32)


def compress_kernel(src_ref, x_ref, o_ref):
    groups = x_ref.shape[1] // (GROUP * TILE)
    zero = jnp.zeros((TILE, TILE), x_ref.dtype)
    i = pl.program_id(0)
    for g in range(groups):
        for s in range(KEEP):
            src = src_ref[(i * groups + g) * KEEP + s]
            cur = zero
            for t in range(GROUP):
                col = (g * GROUP + t) * TILE
                cur = jnp.where(src == t, x_ref[:, col:col + TILE], cur)
            out = (g * KEEP + s) * TILE
            o_ref[:, out:out + TILE] = cur


def compress(x, occ):
    rows, cols = x.shape
    src = tile_of_slot(occ).reshape(-1)
    return pl.pallas_call(
        compress_kernel,
        out_shape=jax.ShapeDtypeStruct((rows, cols * KEEP // GROUP), x.dtype),
        grid_spec=pltpu.PrefetchScalarGridSpec(
            num_scalar_prefetch=1,
            grid=(rows // TILE,),
            in_specs=[pl.BlockSpec((TILE, cols), lambda i, s: (i, 0))],
            out_specs=pl.BlockSpec((TILE, cols * KEEP // GROUP), lambda i, s: (i, 0)),
        ),
    )(src, x)


def product_kernel(k_tiles, finish_square, gblk_ref, rpos_ref, rsel_ref, csel_ref, own_ref, src_ref, rp0_ref,
                   rp1_ref, cpa_ref, cpb_ref, *rest):
    if finish_square:
        o_ref, packed_ref, rpx, cpx, acc = rest
    else:
        sq_ref, o_ref, rpx, cpx, acc = rest
    step = pl.program_id(0)
    step_tiles = cpa_ref.shape[1] // TILE
    row_tiles = rp0_ref.shape[0] // TILE
    col_tiles = o_ref.shape[1] // TILE
    for sub, rp_ref in enumerate((rp0_ref, rp1_ref)):
        block = gblk_ref[2 * step + sub]

        def expand_panel_tile(kt, carry):
            rows = pl.ds(pl.multiple_of(kt * TILE, TILE), TILE)
            dst_rows = pl.ds(pl.multiple_of((sub * step_tiles + kt) * TILE, TILE), TILE)
            for g, cp_ref in enumerate((cpa_ref, cpb_ref)):
                expand_group(cpx, cp_ref.at[sub], csel_ref, ((block * step_tiles + kt) * 2 + g) * GROUP,
                             rows, 0, g, dst_rows=dst_rows)
            return carry

        lax.fori_loop(0, step_tiles, expand_panel_tile, 0)
        for i in range(row_tiles):
            rows = slice(i * TILE, (i + 1) * TILE)
            for q in range(step_tiles // GROUP):
                expand_group(rpx, rp_ref, rsel_ref, i * k_tiles + block * step_tiles + q * GROUP, rows, q,
                             sub * (step_tiles // GROUP) + q)

    @pl.when(step == 0)
    def _():
        acc[...] = jnp.zeros_like(acc)

    acc[...] += jnp.dot(rpx[...], cpx[...], preferred_element_type=jnp.float32)

    @pl.when(step == pl.num_programs(0) - 1)
    def _():
        zero = jnp.zeros((TILE, TILE), jnp.float32)
        for i in range(row_tiles):
            rows = slice(i * TILE, (i + 1) * TILE)
            for j in range(col_tiles):
                cols = slice(j * TILE, (j + 1) * TILE)
                masked = jnp.where(own_ref[i * col_tiles + j] > 0, acc[rows, cols], zero)
                if finish_square:
                    o_ref[rows, cols] = masked.astype(o_ref.dtype)
                else:
                    purified = 3.0 * sq_ref[rows, cols].astype(jnp.float32) - 2.0 * masked
                    o_ref[rows, cols] = purified.astype(o_ref.dtype)
        if finish_square:
            groups = col_tiles // GROUP
            bzero = jnp.zeros((TILE, TILE), o_ref.dtype)
            for i in range(row_tiles):
                rows = slice(i * TILE, (i + 1) * TILE)
                for g in range(groups):
                    for s in range(KEEP):
                        src = src_ref[(i * groups + g) * KEEP + s]
                        cur = bzero
                        for t in range(GROUP):
                            col = (g * GROUP + t) * TILE
                            cur = jnp.where(src == t, o_ref[rows, col:col + TILE], cur)
                        out = (g * KEEP + s) * TILE
                        packed_ref[rows, out:out + TILE] = cur


def expand_group(dst, src_ref, sel_ref, sel_base, rows, src_group, dst_group, dst_rows=None):
    dst_rows = rows if dst_rows is None else dst_rows
    zero = jnp.zeros((TILE, TILE), src_ref.dtype)
    base = src_group * KEEP * TILE
    s0 = src_ref[rows, base:base + TILE]
    s1 = src_ref[rows, base + TILE:base + 2 * TILE]
    for t in range(GROUP):
        sel = sel_ref[sel_base + t]
        col = (dst_group * GROUP + t) * TILE
        dst[dst_rows, col:col + TILE] = jnp.where(sel == 0, s0, jnp.where(sel == 1, s1, zero))


def product(packed_rows, panel_a, panel_b, gblk, rpos, rsel, csel, own, src, square=None):
    blocks, rows, _ = packed_rows.shape
    step_k = panel_a.shape[1]
    cols = 2 * GROUP * TILE
    k_tiles = blocks * step_k // TILE
    index = lambda s, g, p, r, c, o, q: (0, 0)
    in_specs = [
        pl.BlockSpec((None, rows, packed_rows.shape[2]), lambda s, g, p, r, c, o, q: (p[g[2 * s]], 0, 0)),
        pl.BlockSpec((None, rows, packed_rows.shape[2]), lambda s, g, p, r, c, o, q: (p[g[2 * s + 1]], 0, 0)),
        pl.BlockSpec((2, step_k, panel_a.shape[2]), lambda s, g, p, r, c, o, q: (s, 0, 0)),
        pl.BlockSpec((2, step_k, panel_b.shape[2]), lambda s, g, p, r, c, o, q: (s, 0, 0)),
    ]
    operands = [packed_rows, packed_rows, panel_a, panel_b]
    if square is None:
        out_shape = (jax.ShapeDtypeStruct((rows, cols), jnp.bfloat16),
                     jax.ShapeDtypeStruct((rows, cols * KEEP // GROUP), jnp.bfloat16))
        out_specs = (pl.BlockSpec((rows, cols), index), pl.BlockSpec((rows, cols * KEEP // GROUP), index))
    else:
        in_specs.append(pl.BlockSpec((rows, cols), index))
        operands.append(square)
        out_shape = jax.ShapeDtypeStruct((rows, cols), jnp.bfloat16)
        out_specs = pl.BlockSpec((rows, cols), index)
    return pl.pallas_call(
        functools.partial(product_kernel, k_tiles, square is None),
        out_shape=out_shape,
        grid_spec=pltpu.PrefetchScalarGridSpec(
            num_scalar_prefetch=6,
            grid=(blocks // 2,),
            in_specs=in_specs,
            out_specs=out_specs,
            scratch_shapes=[
                pltpu.VMEM((rows, 2 * step_k), packed_rows.dtype),
                pltpu.VMEM((2 * step_k, cols), panel_a.dtype),
                pltpu.VMEM((rows, cols), jnp.float32),
            ],
        ),
        compiler_params=pltpu.CompilerParams(dimension_semantics=("arbitrary",)),
        cost_estimate=pl.CostEstimate(
            flops=2 * rows * blocks * step_k * cols,
            transcendentals=0,
            bytes_accessed=2 * (packed_rows.size + panel_a.size + panel_b.size) + 4 * rows * cols,
        ),
    )(gblk, rpos, rsel, csel, own, src, *operands)


def ring_gather(x, axis, stride=1):
    size = lax.axis_size(axis)
    n = size // stride
    fwd_perm = [(i, (i + stride) % size) for i in range(size)]
    bwd_perm = [(i, (i - stride) % size) for i in range(size)]
    blocks = [None] * n
    blocks[0] = x
    f, b = x, x
    half = n // 2
    for k in range(1, half):
        f = lax.ppermute(f, axis, fwd_perm)
        b = lax.ppermute(b, axis, bwd_perm)
        blocks[n - k] = f
        blocks[k] = b
    if x.size * x.dtype.itemsize <= SMALL_BYTES:
        blocks[half] = lax.ppermute(f, axis, fwd_perm)
        return blocks
    cut = x.shape[0] // 2
    top = lax.ppermute(f[:cut], axis, fwd_perm)
    bottom = lax.ppermute(b[cut:], axis, bwd_perm)
    blocks[half] = jnp.concatenate([top, bottom], axis=0)
    return blocks


def shards(density, pattern):
    row_count, col_width = density.shape
    layers = lax.axis_size("layer")
    cols_n = lax.axis_size("col")
    rows_n = lax.axis_size("row")
    c = lax.axis_index("col")
    l = lax.axis_index("layer")
    r = lax.axis_index("row")
    row_tile0 = (c * layers + l) * (row_count // TILE)
    col_tile0 = r * (col_width // TILE)
    live = pattern > 0
    own_rows = lax.dynamic_slice_in_dim(live, row_tile0, row_count // TILE, axis=0)
    own_cols = lax.dynamic_slice_in_dim(live, col_tile0, col_width // TILE, axis=1)
    own = lax.dynamic_slice_in_dim(own_rows, col_tile0, col_width // TILE, axis=1)

    groups = lambda m: m.reshape(m.shape[0], m.shape[1] // GROUP, GROUP)
    own_occ = groups(own)
    rsel = slot_of_tile(groups(own_rows)).reshape(-1)
    csel = slot_of_tile(groups(own_cols)).reshape(-1)

    packed = compress(density, own_occ)
    width = packed.shape[1] // 2
    part_a, part_b = packed[:, :width], packed[:, width:]
    along_col = jnp.stack(ring_gather(part_a, "col"))
    by_layer = jnp.roll(jnp.stack(ring_gather(along_col, "layer")), l, axis=0)
    panel_a = by_layer.transpose(1, 0, 2, 3).reshape(cols_n, layers * row_count, width)
    by_layer_b = jnp.roll(jnp.stack(ring_gather(part_b, "layer")), l, axis=0)
    piece_b = by_layer_b.reshape(layers * row_count, width)
    panel_b = jnp.stack(ring_gather(piece_b, "col"))

    steps = jnp.arange(cols_n, dtype=jnp.int32)
    gblk = (c + steps) % cols_n

    partner = [(i, i ^ 1) for i in range(rows_n)]
    half_n = rows_n // 2
    held = jnp.concatenate([(r + 2 * steps[:half_n]) % rows_n, ((r ^ 1) + 2 * steps[:half_n]) % rows_n])
    rpos = jnp.sum(jnp.where(held[None, :] == steps[:, None], steps[None, :], 0), axis=1).astype(jnp.int32)

    own_flat = own.astype(jnp.int32).reshape(-1)
    own_src = tile_of_slot(own_occ).reshape(-1)

    def gather_rows(packed):
        mine = jnp.stack(ring_gather(packed, "row", stride=2))
        theirs = lax.ppermute(mine, "row", partner)
        return jnp.concatenate([mine, theirs], axis=0)

    tables = (gblk, rpos, rsel, csel, own_flat, own_src)
    square, packed_square = product(gather_rows(packed), panel_a, panel_b, *tables)
    return product(gather_rows(packed_square), panel_a, panel_b, *tables, square=square)


def solution(mesh):
    return jax.shard_map(
        shards,
        mesh=mesh,
        in_specs=(P(("col", "layer"), "row"), P()),
        out_specs=P(("col", "layer"), "row"),
        check_vma=False,
    )
```

```python
import functools

import jax
import jax.numpy as jnp
from jax import lax
from jax.experimental import pallas as pl
from jax.experimental.pallas import tpu as pltpu
from jax.sharding import PartitionSpec as P

TILE = 128
GROUP = 4
KEEP = 2
SMALL_BYTES = 1 << 17
PER_STEP = 4


def slot_of_tile(occ):
    count = occ.astype(jnp.int32)
    before = jnp.cumsum(count, axis=-1) - count
    return jnp.where(occ, before, KEEP).astype(jnp.int32)


def tile_of_slot(occ):
    slot = slot_of_tile(occ)
    tiles = jnp.arange(GROUP, dtype=jnp.int32)
    picks = [jnp.min(jnp.where(slot == s, tiles, GROUP), axis=-1) for s in range(KEEP)]
    return jnp.stack(picks, axis=-1).astype(jnp.int32)


def compress_kernel(src_ref, x_ref, o_ref):
    groups = x_ref.shape[1] // (GROUP * TILE)
    zero = jnp.zeros((TILE, TILE), x_ref.dtype)
    i = pl.program_id(0)
    for g in range(groups):
        for s in range(KEEP):
            src = src_ref[(i * groups + g) * KEEP + s]
            cur = zero
            for t in range(GROUP):
                col = (g * GROUP + t) * TILE
                cur = jnp.where(src == t, x_ref[:, col:col + TILE], cur)
            out = (g * KEEP + s) * TILE
            o_ref[:, out:out + TILE] = cur


def compress(x, occ):
    rows, cols = x.shape
    src = tile_of_slot(occ).reshape(-1)
    return pl.pallas_call(
        compress_kernel,
        out_shape=jax.ShapeDtypeStruct((rows, cols * KEEP // GROUP), x.dtype),
        grid_spec=pltpu.PrefetchScalarGridSpec(
            num_scalar_prefetch=1,
            grid=(rows // TILE,),
            in_specs=[pl.BlockSpec((TILE, cols), lambda i, s: (i, 0))],
            out_specs=pl.BlockSpec((TILE, cols * KEEP // GROUP), lambda i, s: (i, 0)),
        ),
    )(src, x)


def product_kernel(k_tiles, finish_square, gblk_ref, rpos_ref, rsel_ref, csel_ref, own_ref, src_ref, *refs):
    rp_refs = refs[:PER_STEP]
    cpa_ref, cpb_ref = refs[PER_STEP:PER_STEP + 2]
    rest = refs[PER_STEP + 2:]
    rp0_ref = rp_refs[0]
    if finish_square:
        o_ref, packed_ref, rpx, cpx, acc = rest
    else:
        sq_ref, o_ref, rpx, cpx, acc = rest
    step = pl.program_id(0)
    step_tiles = cpa_ref.shape[1] // TILE
    row_tiles = rp0_ref.shape[0] // TILE
    col_tiles = o_ref.shape[1] // TILE
    for sub, rp_ref in enumerate(rp_refs):
        block = gblk_ref[PER_STEP * step + sub]

        def expand_panel_tile(kt, carry):
            rows = pl.ds(pl.multiple_of(kt * TILE, TILE), TILE)
            dst_rows = pl.ds(pl.multiple_of((sub * step_tiles + kt) * TILE, TILE), TILE)
            for g, cp_ref in enumerate((cpa_ref, cpb_ref)):
                expand_group(cpx, cp_ref.at[sub], csel_ref, ((block * step_tiles + kt) * 2 + g) * GROUP,
                             rows, 0, g, dst_rows=dst_rows)
            return carry

        lax.fori_loop(0, step_tiles, expand_panel_tile, 0)
        for i in range(row_tiles):
            rows = slice(i * TILE, (i + 1) * TILE)
            for q in range(step_tiles // GROUP):
                expand_group(rpx, rp_ref, rsel_ref, i * k_tiles + block * step_tiles + q * GROUP, rows, q,
                             sub * (step_tiles // GROUP) + q)

    @pl.when(step == 0)
    def _():
        acc[...] = jnp.zeros_like(acc)

    acc[...] += jnp.dot(rpx[...], cpx[...], preferred_element_type=jnp.float32)

    @pl.when(step == pl.num_programs(0) - 1)
    def _():
        zero = jnp.zeros((TILE, TILE), jnp.float32)
        for i in range(row_tiles):
            rows = slice(i * TILE, (i + 1) * TILE)
            for j in range(col_tiles):
                cols = slice(j * TILE, (j + 1) * TILE)
                masked = jnp.where(own_ref[i * col_tiles + j] > 0, acc[rows, cols], zero)
                if finish_square:
                    o_ref[rows, cols] = masked.astype(o_ref.dtype)
                else:
                    purified = 3.0 * sq_ref[rows, cols].astype(jnp.float32) - 2.0 * masked
                    o_ref[rows, cols] = purified.astype(o_ref.dtype)
        if finish_square:
            groups = col_tiles // GROUP
            bzero = jnp.zeros((TILE, TILE), o_ref.dtype)
            for i in range(row_tiles):
                rows = slice(i * TILE, (i + 1) * TILE)
                for g in range(groups):
                    for s in range(KEEP):
                        src = src_ref[(i * groups + g) * KEEP + s]
                        cur = bzero
                        for t in range(GROUP):
                            col = (g * GROUP + t) * TILE
                            cur = jnp.where(src == t, o_ref[rows, col:col + TILE], cur)
                        out = (g * KEEP + s) * TILE
                        packed_ref[rows, out:out + TILE] = cur


def expand_group(dst, src_ref, sel_ref, sel_base, rows, src_group, dst_group, dst_rows=None):
    dst_rows = rows if dst_rows is None else dst_rows
    zero = jnp.zeros((TILE, TILE), src_ref.dtype)
    base = src_group * KEEP * TILE
    s0 = src_ref[rows, base:base + TILE]
    s1 = src_ref[rows, base + TILE:base + 2 * TILE]
    for t in range(GROUP):
        sel = sel_ref[sel_base + t]
        col = (dst_group * GROUP + t) * TILE
        dst[dst_rows, col:col + TILE] = jnp.where(sel == 0, s0, jnp.where(sel == 1, s1, zero))


def product(packed_rows, panel_a, panel_b, gblk, rpos, rsel, csel, own, src, square=None):
    blocks, rows, _ = packed_rows.shape
    step_k = panel_a.shape[1]
    cols = 2 * GROUP * TILE
    k_tiles = blocks * step_k // TILE
    index = lambda s, g, p, r, c, o, q: (0, 0)
    in_specs = [
        pl.BlockSpec((None, rows, packed_rows.shape[2]),
                     functools.partial(lambda sub, s, g, p, r, c, o, q: (p[g[PER_STEP * s + sub]], 0, 0), sub))
        for sub in range(PER_STEP)
    ] + [
        pl.BlockSpec((PER_STEP, step_k, panel_a.shape[2]), lambda s, g, p, r, c, o, q: (s, 0, 0)),
        pl.BlockSpec((PER_STEP, step_k, panel_b.shape[2]), lambda s, g, p, r, c, o, q: (s, 0, 0)),
    ]
    operands = [packed_rows] * PER_STEP + [panel_a, panel_b]
    if square is None:
        out_shape = (jax.ShapeDtypeStruct((rows, cols), jnp.bfloat16),
                     jax.ShapeDtypeStruct((rows, cols * KEEP // GROUP), jnp.bfloat16))
        out_specs = (pl.BlockSpec((rows, cols), index), pl.BlockSpec((rows, cols * KEEP // GROUP), index))
    else:
        in_specs.append(pl.BlockSpec((rows, cols), index))
        operands.append(square)
        out_shape = jax.ShapeDtypeStruct((rows, cols), jnp.bfloat16)
        out_specs = pl.BlockSpec((rows, cols), index)
    return pl.pallas_call(
        functools.partial(product_kernel, k_tiles, square is None),
        out_shape=out_shape,
        grid_spec=pltpu.PrefetchScalarGridSpec(
            num_scalar_prefetch=6,
            grid=(blocks // PER_STEP,),
            in_specs=in_specs,
            out_specs=out_specs,
            scratch_shapes=[
                pltpu.VMEM((rows, PER_STEP * step_k), packed_rows.dtype),
                pltpu.VMEM((PER_STEP * step_k, cols), panel_a.dtype),
                pltpu.VMEM((rows, cols), jnp.float32),
            ],
        ),
        compiler_params=pltpu.CompilerParams(dimension_semantics=("arbitrary",)),
        cost_estimate=pl.CostEstimate(
            flops=2 * rows * blocks * step_k * cols,
            transcendentals=0,
            bytes_accessed=2 * (packed_rows.size + panel_a.size + panel_b.size) + 4 * rows * cols,
        ),
    )(gblk, rpos, rsel, csel, own, src, *operands)


def ring_gather(x, axis, stride=1):
    size = lax.axis_size(axis)
    n = size // stride
    fwd_perm = [(i, (i + stride) % size) for i in range(size)]
    bwd_perm = [(i, (i - stride) % size) for i in range(size)]
    blocks = [None] * n
    blocks[0] = x
    f, b = x, x
    half = n // 2
    for k in range(1, half):
        f = lax.ppermute(f, axis, fwd_perm)
        b = lax.ppermute(b, axis, bwd_perm)
        blocks[n - k] = f
        blocks[k] = b
    if x.size * x.dtype.itemsize <= SMALL_BYTES:
        blocks[half] = lax.ppermute(f, axis, fwd_perm)
        return blocks
    cut = x.shape[0] // 2
    top = lax.ppermute(f[:cut], axis, fwd_perm)
    bottom = lax.ppermute(b[cut:], axis, bwd_perm)
    blocks[half] = jnp.concatenate([top, bottom], axis=0)
    return blocks


def shards(density, pattern):
    row_count, col_width = density.shape
    layers = lax.axis_size("layer")
    cols_n = lax.axis_size("col")
    rows_n = lax.axis_size("row")
    c = lax.axis_index("col")
    l = lax.axis_index("layer")
    r = lax.axis_index("row")
    row_tile0 = (c * layers + l) * (row_count // TILE)
    col_tile0 = r * (col_width // TILE)
    live = pattern > 0
    own_rows = lax.dynamic_slice_in_dim(live, row_tile0, row_count // TILE, axis=0)
    own_cols = lax.dynamic_slice_in_dim(live, col_tile0, col_width // TILE, axis=1)
    own = lax.dynamic_slice_in_dim(own_rows, col_tile0, col_width // TILE, axis=1)

    groups = lambda m: m.reshape(m.shape[0], m.shape[1] // GROUP, GROUP)
    own_occ = groups(own)
    rsel = slot_of_tile(groups(own_rows)).reshape(-1)
    csel = slot_of_tile(groups(own_cols)).reshape(-1)

    packed = compress(density, own_occ)
    width = packed.shape[1] // 2
    part_a, part_b = packed[:, :width], packed[:, width:]
    along_col = jnp.stack(ring_gather(part_a, "col"))
    by_layer = jnp.roll(jnp.stack(ring_gather(along_col, "layer")), l, axis=0)
    panel_a = by_layer.transpose(1, 0, 2, 3).reshape(cols_n, layers * row_count, width)
    by_layer_b = jnp.roll(jnp.stack(ring_gather(part_b, "layer")), l, axis=0)
    piece_b = by_layer_b.reshape(layers * row_count, width)
    panel_b = jnp.stack(ring_gather(piece_b, "col"))

    steps = jnp.arange(cols_n, dtype=jnp.int32)
    gblk = (c + steps) % cols_n

    partner = [(i, i ^ 1) for i in range(rows_n)]
    half_n = rows_n // 2
    held = jnp.concatenate([(r + 2 * steps[:half_n]) % rows_n, ((r ^ 1) + 2 * steps[:half_n]) % rows_n])
    rpos = jnp.sum(jnp.where(held[None, :] == steps[:, None], steps[None, :], 0), axis=1).astype(jnp.int32)

    own_flat = own.astype(jnp.int32).reshape(-1)
    own_src = tile_of_slot(own_occ).reshape(-1)

    def gather_rows(packed):
        mine = jnp.stack(ring_gather(packed, "row", stride=2))
        theirs = lax.ppermute(mine, "row", partner)
        return jnp.concatenate([mine, theirs], axis=0)

    tables = (gblk, rpos, rsel, csel, own_flat, own_src)
    square, packed_square = product(gather_rows(packed), panel_a, panel_b, *tables)
    return product(gather_rows(packed_square), panel_a, panel_b, *tables, square=square)


def solution(mesh):
    return jax.shard_map(
        shards,
        mesh=mesh,
        in_specs=(P(("col", "layer"), "row"), P()),
        out_specs=P(("col", "layer"), "row"),
        check_vma=False,
    )
```
